128 devices in a mesh: prow: 8 (over x_hi, z), pcol: 16 (over x_lo, y, core).
Axes of the slice: x: 4 (x_hi: 2, x_lo: 2; x = x_hi * 2 + x_lo), y: 4, z: 4, core: 2. Of those that a mesh axis runs over, the one named last changes fastest.
Arguments:
- left_vecs: bfloat16 [65536, 4096], P(('prow', 'pcol'))
- right_vecs: bfloat16 [65536, 4096], P(('prow', 'pcol'))
- primal: bfloat16 [4096, 4096], P(('prow', 'pcol'))
- dual_inverse: bfloat16 [4096, 4096], P(('prow', 'pcol'))
- owner_map: int32 [128], replicated, may hold values from 0 to 127, each once
- panel_index: int32 [1], replicated, may hold values from 0 to 254
Outputs:
- panel_factor: float32 [256, 65536], P('pcol', 'prow')
- ahead_update: float32 [256, 65536], P('pcol', 'prow')
The draws below stay inside these ranges and needn't reach their ends.
All inputs are finite; a program needn't handle non-finite values.
Results may differ from the reference program's by a relative error of at most 0.00067.
Values may be sent and summed in bfloat16 or wider, within the bound.
No kernel may reach another device: no remote copies, remote signals or barrier semaphores. Data moves between devices by JAX's collectives and lax.ppermute only.
A program may use at most 128 MiB of HBM per device.

```python
import math
import jax
import jax.numpy as jnp
from jax import lax

ORDER = 4096
PANEL = 256
CON_DEV = 512
CONSTRAINTS = 65536
N_PROW = 8
N_PCOL = 16


def symmetric_draw(key, salt):
    keys = jax.random.split(jax.random.fold_in(key, salt), 2)
    diagonal = jax.random.uniform(keys[0], (ORDER,), jnp.float32, 2.0, 4.0)
    noise = jax.random.normal(keys[1], (ORDER, ORDER), jnp.float32)
    symmetric = (noise + noise.T) * (0.35 / math.sqrt(ORDER))
    return (symmetric + jnp.diag(diagonal)).astype(jnp.bfloat16)


def draw_primal(key, part):
    return symmetric_draw(key, 17)


def draw_dual_inverse(key, part):
    return symmetric_draw(key, 29)


def unit_draw(key, shape):
    return jax.random.normal(key, shape, jnp.float32)


def constraint_draw(key, salt):
    shared_key = jax.random.fold_in(key, 101)
    member_keys = jax.random.split(jax.random.fold_in(key, salt), 2)
    scale = 1.0 / math.sqrt(ORDER)
    directions = unit_draw(shared_key, (8, ORDER)) * scale
    weights_mix = unit_draw(member_keys[0], (CONSTRAINTS, 8)) * (1.0 / math.sqrt(8.0))
    mixed = unit_draw(member_keys[1], (CONSTRAINTS, ORDER)) * (0.7 * scale)
    for direction_num in range(8):
        mixed = mixed + 0.7 * weights_mix[:, direction_num:direction_num + 1] * directions[direction_num][None, :]
    limit = 6.0 * scale
    return jnp.clip(mixed, -limit, limit).astype(jnp.bfloat16)


def draw_left_vecs(key, part):
    return constraint_draw(key, 11)


def draw_right_vecs(key, part):
    return constraint_draw(key, 13)


def setup_inputs(seed: int = 0) -> dict:
    key_of = jax.random.split(jax.random.key(seed), 7)
    left_vecs = draw_left_vecs(jax.random.fold_in(key_of[6], 71), 0)
    right_vecs = draw_right_vecs(jax.random.fold_in(key_of[6], 71), 0)
    primal = draw_primal(jax.random.fold_in(key_of[6], 71), 0)
    dual_inverse = draw_dual_inverse(jax.random.fold_in(key_of[6], 71), 0)
    owner_map = jax.random.permutation(key_of[4], N_PROW * N_PCOL).astype(jnp.int32)
    panel_index = jax.random.randint(key_of[5], (1,), 0, CONSTRAINTS // PANEL - 1).astype(jnp.int32)
    return {"left_vecs": left_vecs, "right_vecs": right_vecs, "primal": primal, "dual_inverse": dual_inverse, "owner_map": owner_map, "panel_index": panel_index}


def combine(left_prod, right_prod):
    seg = 2 * PANEL
    return left_prod[:, seg:2 * seg] * right_prod[:, 2 * seg:3 * seg] + right_prod[:, seg:2 * seg] * left_prod[:, 2 * seg:3 * seg] + left_prod[:, 0:seg] * right_prod[:, 3 * seg:4 * seg] + right_prod[:, 0:seg] * left_prod[:, 3 * seg:4 * seg]

def cyclic(matrix):
    blocks = CONSTRAINTS // (PANEL * N_PROW)
    return matrix.reshape(blocks, N_PROW, PANEL, PANEL).transpose(1, 0, 2, 3).reshape(CONSTRAINTS, PANEL).T

def reference(left_vecs, right_vecs, primal, dual_inverse, owner_map, panel_index):
    devices = N_PROW * N_PCOL
    order_idx = jnp.arange(CONSTRAINTS, dtype=jnp.int32)
    sources = (jnp.take(owner_map, order_idx % devices) * CON_DEV + order_idx // devices).astype(jnp.int32)
    start = (panel_index[0] * PANEL).astype(jnp.int32)
    zero_idx = jnp.zeros((), jnp.int32)
    picked = jnp.take(sources, start + jnp.arange(2 * PANEL, dtype=jnp.int32))
    vectors = jnp.concatenate([jnp.take(left_vecs, picked, axis=0), jnp.take(right_vecs, picked, axis=0)], axis=0)
    primal_img = jnp.dot(primal.astype(jnp.float32), vectors.T.astype(jnp.float32), preferred_element_type=jnp.float32)
    dual_img = jnp.dot(dual_inverse.astype(jnp.float32), vectors.T.astype(jnp.float32), preferred_element_type=jnp.float32)
    images = jnp.concatenate([primal_img, dual_img], axis=1).astype(jnp.bfloat16)

    def form(block):
        begin = (block * CON_DEV).astype(jnp.int32)
        rows = lax.dynamic_slice_in_dim(sources, begin, CON_DEV)
        left_prod = jnp.dot(jnp.take(left_vecs, rows, axis=0).astype(jnp.float32), images.astype(jnp.float32), preferred_element_type=jnp.float32)
        right_prod = jnp.dot(jnp.take(right_vecs, rows, axis=0).astype(jnp.float32), images.astype(jnp.float32), preferred_element_type=jnp.float32)
        return combine(left_prod, right_prod)
    schur = lax.map(form, jnp.arange(devices, dtype=jnp.int32)).reshape(CONSTRAINTS, 2 * PANEL)
    base = lax.dynamic_slice(schur, (start, zero_idx), (PANEL, PANEL))
    chol = jnp.linalg.cholesky(base)
    inverse = lax.linalg.triangular_solve(chol, jnp.eye(PANEL, dtype=jnp.float32), left_side=True, lower=True)
    full = jnp.dot(schur[:, :PANEL].astype(jnp.float32), inverse.T.astype(jnp.float32), precision=lax.Precision.HIGHEST, preferred_element_type=jnp.float32)
    full = jnp.where((order_idx >= start)[:, None], full, jnp.float32(0.0))
    ahead_start = (start + PANEL).astype(jnp.int32)
    ahead = lax.dynamic_slice(full, (ahead_start, zero_idx), (PANEL, PANEL))
    update = schur[:, PANEL:] - jnp.dot(full.astype(jnp.float32), ahead.T.astype(jnp.float32), precision=lax.Precision.HIGHEST, preferred_element_type=jnp.float32)
    update = jnp.where((order_idx >= ahead_start)[:, None], update, jnp.float32(0.0))
    return (cyclic(full), cyclic(update))
```

```python
import jax
import jax.numpy as jnp
from jax import lax
from jax.sharding import PartitionSpec as P

PANEL = 256


def combine(left_prod, right_prod):
    seg = 2 * PANEL
    return (
        left_prod[:, seg : 2 * seg] * right_prod[:, 2 * seg : 3 * seg]
        + right_prod[:, seg : 2 * seg] * left_prod[:, 2 * seg : 3 * seg]
        + left_prod[:, 0:seg] * right_prod[:, 3 * seg : 4 * seg]
        + right_prod[:, 0:seg] * left_prod[:, 3 * seg : 4 * seg]
    )


def gather_all(x):
    x = lax.all_gather(x, "pcol", axis=0, tiled=True)
    return lax.all_gather(x, "prow", axis=0, tiled=True)


def relay_rows(first_part, second_part, owner_map, devices, grid_rows):
    slots = first_part.shape[0]
    height = PANEL // devices
    groups = slots // (grid_rows * height)
    grid_cols = devices // grid_rows
    narrow = PANEL // grid_cols
    stacked = jnp.stack([first_part, second_part], axis=1)
    stacked = stacked.reshape(groups, grid_rows, height, 2, grid_cols, narrow)
    outgoing = stacked.transpose(1, 4, 3, 5, 0, 2).reshape(devices, 2 * narrow * groups * height)
    arrived = lax.all_to_all(outgoing, ("prow", "pcol"), split_axis=0, concat_axis=0, tiled=True)
    ordered = jnp.take(arrived, owner_map, axis=0)
    ordered = ordered.reshape(devices, 2, narrow, groups, height)
    placed = ordered.transpose(1, 2, 3, 4, 0).reshape(2, narrow, groups * height * devices)
    return (placed[0], placed[1])


def body(left_vecs, right_vecs, primal, dual_inverse, owner_map, panel_index):
    devices = lax.axis_size(("prow", "pcol"))
    grid_rows = lax.axis_size("prow")
    grid_cols = lax.axis_size("pcol")
    per_device = 2 * PANEL // devices
    start = panel_index[0] * PANEL
    first_slot = start // devices
    me = lax.axis_index("prow") * grid_cols + lax.axis_index("pcol")
    residue = jnp.sum(jnp.where(owner_map == me, jnp.arange(devices, dtype=jnp.int32), 0))
    panel_left = lax.dynamic_slice_in_dim(left_vecs, first_slot, per_device, 0)
    panel_right = lax.dynamic_slice_in_dim(right_vecs, first_slot, per_device, 0)
    panel_pairs = jnp.stack([panel_left, panel_right], axis=1)
    matrices = jnp.stack([primal, dual_inverse], axis=0)
    raw_images = jnp.einsum(
        "gfn,mcn->gfmc",
        matrices,
        gather_all(panel_pairs),
        preferred_element_type=jnp.float32,
    )
    column_ids = jnp.arange(2 * PANEL, dtype=jnp.int32)
    gathered_ids = jnp.take(owner_map, column_ids % devices) * per_device + column_ids // devices
    ordered = jnp.take(raw_images, gathered_ids, axis=2)
    feature_rows = ordered.shape[1]
    images = ordered.transpose(1, 0, 3, 2).reshape(feature_rows, 8 * PANEL).astype(jnp.bfloat16)
    piece = gather_all(images)
    left_prod = jnp.dot(left_vecs, piece, preferred_element_type=jnp.float32)
    right_prod = jnp.dot(right_vecs, piece, preferred_element_type=jnp.float32)
    schur = combine(left_prod, right_prod)
    own_panel = lax.dynamic_slice_in_dim(schur[:, :PANEL], first_slot, per_device, 0)
    panel_block = gather_all(own_panel)
    panel_block = jnp.take(panel_block, gathered_ids, axis=0)
    chol = jnp.linalg.cholesky(panel_block[:PANEL])
    inverse = lax.linalg.triangular_solve(
        chol, jnp.eye(PANEL, dtype=jnp.float32), left_side=True, lower=True
    )
    ahead = jnp.dot(
        panel_block[PANEL:],
        inverse.T,
        precision=lax.Precision.HIGHEST,
        preferred_element_type=jnp.float32,
    )
    slots = schur.shape[0]
    schur_ids = jnp.arange(slots, dtype=jnp.int32) * devices + residue
    full = jnp.dot(
        schur[:, :PANEL],
        inverse.T,
        precision=lax.Precision.HIGHEST,
        preferred_element_type=jnp.float32,
    )
    full = jnp.where((schur_ids >= start)[:, None], full, jnp.float32(0.0))
    update = schur[:, PANEL:] - jnp.dot(
        full, ahead.T, precision=lax.Precision.HIGHEST, preferred_element_type=jnp.float32
    )
    update = jnp.where((schur_ids >= start + PANEL)[:, None], update, jnp.float32(0.0))
    return relay_rows(full, update, owner_map, devices, grid_rows)


def solution(mesh):
    return jax.shard_map(
        body,
        mesh=mesh,
        in_specs=(
            P(("prow", "pcol"), None),
            P(("prow", "pcol"), None),
            P(("prow", "pcol"), None),
            P(("prow", "pcol"), None),
            P(),
            P(),
        ),
        out_specs=(P("pcol", "prow"), P("pcol", "prow")),
        check_vma=False,
    )
```

```python
import jax
import jax.numpy as jnp
from jax import lax
from jax.sharding import PartitionSpec as P

PANEL = 256


def combine(left_prod, right_prod):
    seg = left_prod.shape[1] // 4
    return (
        left_prod[:, seg : 2 * seg] * right_prod[:, 2 * seg : 3 * seg]
        + right_prod[:, seg : 2 * seg] * left_prod[:, 2 * seg : 3 * seg]
        + left_prod[:, 0:seg] * right_prod[:, 3 * seg : 4 * seg]
        + right_prod[:, 0:seg] * left_prod[:, 3 * seg : 4 * seg]
    )


def gather_all(x):
    x = lax.all_gather(x, "prow", axis=0, tiled=True)
    return lax.all_gather(x, "pcol", axis=0, tiled=True)


def relay_rows(first_part, second_part, owner_map, devices, grid_rows):
    slots = first_part.shape[0]
    height = PANEL // devices
    groups = slots // (grid_rows * height)
    grid_cols = devices // grid_rows
    narrow = PANEL // grid_cols
    stacked = jnp.stack([first_part, second_part], axis=1)
    stacked = stacked.reshape(groups, grid_rows, height, 2, grid_cols, narrow)
    outgoing = stacked.transpose(1, 4, 3, 5, 0, 2).reshape(devices, 2 * narrow * groups * height)
    arrived = lax.all_to_all(outgoing, ("prow", "pcol"), split_axis=0, concat_axis=0, tiled=True)
    ordered = jnp.take(arrived, owner_map, axis=0)
    ordered = ordered.reshape(devices, 2, narrow, groups, height)
    placed = ordered.transpose(1, 2, 3, 4, 0).reshape(2, narrow, groups * height * devices)
    return (placed[0], placed[1])


def body(left_vecs, right_vecs, primal, dual_inverse, owner_map, panel_index):
    devices = lax.axis_size(("prow", "pcol"))
    grid_rows = lax.axis_size("prow")
    grid_cols = lax.axis_size("pcol")
    per_device = 2 * PANEL // devices
    start = panel_index[0] * PANEL
    first_slot = start // devices
    me = lax.axis_index("prow") * grid_cols + lax.axis_index("pcol")
    residue = jnp.sum(jnp.where(owner_map == me, jnp.arange(devices, dtype=jnp.int32), 0))
    panel_left = lax.dynamic_slice_in_dim(left_vecs, first_slot, per_device, 0)
    panel_right = lax.dynamic_slice_in_dim(right_vecs, first_slot, per_device, 0)
    panel_pairs = jnp.stack([panel_left, panel_right], axis=1)
    matrices = jnp.stack([primal, dual_inverse], axis=0)
    gathered_pairs = gather_all(panel_pairs)
    raw_images = jnp.einsum(
        "gfn,mcn->gfmc", matrices, gathered_pairs, preferred_element_type=jnp.float32
    )
    column_ids = jnp.arange(2 * PANEL, dtype=jnp.int32)
    owners = jnp.take(owner_map, column_ids % devices)
    gathered_ids = (
        (owners % grid_cols) * grid_rows + owners // grid_cols
    ) * per_device + column_ids // devices
    ordered = jnp.take(raw_images, gathered_ids, axis=2)
    feature_rows = ordered.shape[1]
    images = ordered.transpose(1, 0, 3, 2).reshape(feature_rows, 8 * PANEL).astype(jnp.bfloat16)
    piece = gather_all(images)

    def feature_order(vecs):
        rows = vecs.shape[0]
        vecs = vecs.reshape(rows, grid_rows, grid_cols, feature_rows)
        return vecs.transpose(0, 2, 1, 3).reshape(rows, grid_rows * grid_cols * feature_rows)

    left_prod = jnp.dot(feature_order(left_vecs), piece, preferred_element_type=jnp.float32)
    right_prod = jnp.dot(feature_order(right_vecs), piece, preferred_element_type=jnp.float32)
    schur = combine(left_prod, right_prod)
    panel_vecs = jnp.take(gathered_pairs, gathered_ids, axis=0)
    half = piece.reshape(piece.shape[0], 4, 2 * PANEL)[:, :, :PANEL].reshape(piece.shape[0], 4 * PANEL)
    panel_block = combine(
        jnp.dot(feature_order(panel_vecs[:, 0]), half, preferred_element_type=jnp.float32),
        jnp.dot(feature_order(panel_vecs[:, 1]), half, preferred_element_type=jnp.float32),
    )
    chol = jnp.linalg.cholesky(panel_block[:PANEL])
    inverse = lax.linalg.triangular_solve(
        chol, jnp.eye(PANEL, dtype=jnp.float32), left_side=True, lower=True
    )
    ahead = jnp.dot(
        panel_block[PANEL:],
        inverse.T,
        precision=lax.Precision.HIGHEST,
        preferred_element_type=jnp.float32,
    )
    slots = schur.shape[0]
    schur_ids = jnp.arange(slots, dtype=jnp.int32) * devices + residue
    full = jnp.dot(
        schur[:, :PANEL],
        inverse.T,
        precision=lax.Precision.HIGHEST,
        preferred_element_type=jnp.float32,
    )
    full = jnp.where((schur_ids >= start)[:, None], full, jnp.float32(0.0))
    update = schur[:, PANEL:] - jnp.dot(
        full, ahead.T, precision=lax.Precision.HIGHEST, preferred_element_type=jnp.float32
    )
    update = jnp.where((schur_ids >= start + PANEL)[:, None], update, jnp.float32(0.0))
    return relay_rows(full, update, owner_map, devices, grid_rows)


def solution(mesh):
    return jax.shard_map(
        body,
        mesh=mesh,
        in_specs=(
            P(("prow", "pcol"), None),
            P(("prow", "pcol"), None),
            P(("prow", "pcol"), None),
            P(("prow", "pcol"), None),
            P(),
            P(),
        ),
        out_specs=(P("pcol", "prow"), P("pcol", "prow")),
        check_vma=False,
    )
```

```python
import jax
import jax.numpy as jnp
from jax import lax
from jax.sharding import PartitionSpec as P

PANEL = 256


def combine(left_prod, right_prod):
    seg = left_prod.shape[1] // 4
    return (
        left_prod[:, seg : 2 * seg] * right_prod[:, 2 * seg : 3 * seg]
        + right_prod[:, seg : 2 * seg] * left_prod[:, 2 * seg : 3 * seg]
        + left_prod[:, 0:seg] * right_prod[:, 3 * seg : 4 * seg]
        + right_prod[:, 0:seg] * left_prod[:, 3 * seg : 4 * seg]
    )


def gather_all(x):
    x = lax.all_gather(x, "prow", axis=0, tiled=True)
    return lax.all_gather(x, "pcol", axis=0, tiled=True)


def relay_rows(first_part, second_part, owner_map, devices, grid_rows):
    slots = first_part.shape[0]
    height = PANEL // devices
    groups = slots // (grid_rows * height)
    grid_cols = devices // grid_rows
    narrow = PANEL // grid_cols
    stacked = jnp.stack([first_part, second_part], axis=1)
    stacked = stacked.reshape(groups, grid_rows, height, 2, grid_cols, narrow)
    outgoing = stacked.transpose(1, 4, 3, 5, 0, 2).reshape(devices, 2 * narrow * groups * height)
    arrived = lax.all_to_all(outgoing, ("prow", "pcol"), split_axis=0, concat_axis=0, tiled=True)
    ordered = jnp.take(arrived, owner_map, axis=0)
    ordered = ordered.reshape(devices, 2, narrow, groups, height)
    placed = ordered.transpose(1, 2, 3, 4, 0).reshape(2, narrow, groups * height * devices)
    return (placed[0], placed[1])


def body(left_vecs, right_vecs, primal, dual_inverse, owner_map, panel_index):
    devices = lax.axis_size(("prow", "pcol"))
    grid_rows = lax.axis_size("prow")
    grid_cols = lax.axis_size("pcol")
    per_device = 2 * PANEL // devices
    start = panel_index[0] * PANEL
    first_slot = start // devices
    me = lax.axis_index("prow") * grid_cols + lax.axis_index("pcol")
    residue = jnp.sum(jnp.where(owner_map == me, jnp.arange(devices, dtype=jnp.int32), 0))
    panel_left = lax.dynamic_slice_in_dim(left_vecs, first_slot, per_device, 0)
    panel_right = lax.dynamic_slice_in_dim(right_vecs, first_slot, per_device, 0)
    panel_pairs = jnp.stack([panel_left, panel_right], axis=1)
    moves = [
        ((q * grid_rows + p), (p * grid_cols + q))
        for p in range(grid_rows)
        for q in range(grid_cols)
    ]
    matrices = lax.ppermute(
        jnp.stack([primal, dual_inverse], axis=0), ("prow", "pcol"), perm=moves
    )
    gathered_pairs = gather_all(panel_pairs)
    raw_images = jnp.einsum(
        "gfn,mcn->gfmc", matrices, gathered_pairs, preferred_element_type=jnp.float32
    )
    column_ids = jnp.arange(2 * PANEL, dtype=jnp.int32)
    owners = jnp.take(owner_map, column_ids % devices)
    gathered_ids = (
        (owners % grid_cols) * grid_rows + owners // grid_cols
    ) * per_device + column_ids // devices
    ordered = jnp.take(raw_images, gathered_ids, axis=2)
    feature_rows = ordered.shape[1]
    images = ordered.transpose(1, 0, 3, 2).reshape(feature_rows, 8 * PANEL).astype(jnp.bfloat16)
    piece = gather_all(images)
    left_prod = jnp.dot(left_vecs, piece, preferred_element_type=jnp.float32)
    right_prod = jnp.dot(right_vecs, piece, preferred_element_type=jnp.float32)
    schur = combine(left_prod, right_prod)
    panel_vecs = jnp.take(gathered_pairs, gathered_ids, axis=0)
    panel_block = combine(
        jnp.dot(panel_vecs[:, 0], piece, preferred_element_type=jnp.float32),
        jnp.dot(panel_vecs[:, 1], piece, preferred_element_type=jnp.float32),
    )[:, :PANEL]
    chol = jnp.linalg.cholesky(panel_block[:PANEL])
    inverse = lax.linalg.triangular_solve(
        chol, jnp.eye(PANEL, dtype=jnp.float32), left_side=True, lower=True
    )
    ahead = jnp.dot(
        panel_block[PANEL:],
        inverse.T,
        precision=lax.Precision.HIGHEST,
        preferred_element_type=jnp.float32,
    )
    slots = schur.shape[0]
    schur_ids = jnp.arange(slots, dtype=jnp.int32) * devices + residue
    full = jnp.dot(
        schur[:, :PANEL],
        inverse.T,
        precision=lax.Precision.HIGHEST,
        preferred_element_type=jnp.float32,
    )
    full = jnp.where((schur_ids >= start)[:, None], full, jnp.float32(0.0))
    update = schur[:, PANEL:] - jnp.dot(
        full, ahead.T, precision=lax.Precision.HIGHEST, preferred_element_type=jnp.float32
    )
    update = jnp.where((schur_ids >= start + PANEL)[:, None], update, jnp.float32(0.0))
    return relay_rows(full, update, owner_map, devices, grid_rows)


def solution(mesh):
    return jax.shard_map(
        body,
        mesh=mesh,
        in_specs=(
            P(("prow", "pcol"), None),
            P(("prow", "pcol"), None),
            P(("prow", "pcol"), None),
            P(("prow", "pcol"), None),
            P(),
            P(),
        ),
        out_specs=(P("pcol", "prow"), P("pcol", "prow")),
        check_vma=False,
    )
```

```python
import jax
import jax.numpy as jnp
from jax import lax
from jax.sharding import PartitionSpec as P

PANEL = 256


def combine(left_prod, right_prod):
    seg = left_prod.shape[1] // 4
    return (
        left_prod[:, seg : 2 * seg] * right_prod[:, 2 * seg : 3 * seg]
        + right_prod[:, seg : 2 * seg] * left_prod[:, 2 * seg : 3 * seg]
        + left_prod[:, 0:seg] * right_prod[:, 3 * seg : 4 * seg]
        + right_prod[:, 0:seg] * left_prod[:, 3 * seg : 4 * seg]
    )


def gather_prow(x):
    size = lax.axis_size("prow")
    me = lax.axis_index("prow")
    step = 1
    while step < size:
        got = lax.ppermute(x, "prow", perm=[(i, i ^ step) for i in range(size)])
        low = (me & step) == 0
        x = jnp.where(low, jnp.concatenate([x, got], axis=0), jnp.concatenate([got, x], axis=0))
        step *= 2
    return x


def gather_all(x):
    return lax.all_gather(gather_prow(x), "pcol", axis=0, tiled=True)


def relay_rows(first_part, second_part, owner_map, devices, grid_rows):
    slots = first_part.shape[0]
    height = PANEL // devices
    groups = slots // (grid_rows * height)
    grid_cols = devices // grid_rows
    narrow = PANEL // grid_cols
    stacked = jnp.stack([first_part, second_part], axis=1)
    stacked = stacked.reshape(groups, grid_rows, height, 2, grid_cols, narrow)
    outgoing = stacked.transpose(1, 4, 3, 5, 0, 2).reshape(devices, 2 * narrow * groups * height)
    arrived = lax.all_to_all(outgoing, ("prow", "pcol"), split_axis=0, concat_axis=0, tiled=True)
    ordered = jnp.take(arrived, owner_map, axis=0)
    ordered = ordered.reshape(devices, 2, narrow, groups, height)
    placed = ordered.transpose(1, 2, 3, 4, 0).reshape(2, narrow, groups * height * devices)
    return (placed[0], placed[1])


def body(left_vecs, right_vecs, primal, dual_inverse, owner_map, panel_index):
    devices = lax.axis_size(("prow", "pcol"))
    grid_rows = lax.axis_size("prow")
    grid_cols = lax.axis_size("pcol")
    per_device = 2 * PANEL // devices
    start = panel_index[0] * PANEL
    first_slot = start // devices
    me = lax.axis_index("prow") * grid_cols + lax.axis_index("pcol")
    residue = jnp.sum(jnp.where(owner_map == me, jnp.arange(devices, dtype=jnp.int32), 0))
    panel_left = lax.dynamic_slice_in_dim(left_vecs, first_slot, per_device, 0)
    panel_right = lax.dynamic_slice_in_dim(right_vecs, first_slot, per_device, 0)
    panel_pairs = jnp.concatenate([panel_left, panel_right], axis=0)
    moves = [
        ((q * grid_rows + p), (p * grid_cols + q))
        for p in range(grid_rows)
        for q in range(grid_cols)
    ]
    matrices = lax.ppermute(
        jnp.stack([primal, dual_inverse], axis=0), ("prow", "pcol"), perm=moves
    )
    gathered_pairs = gather_all(panel_pairs)
    raw_images = jnp.einsum(
        "gfn,mn->gfm", matrices, gathered_pairs, preferred_element_type=jnp.float32
    )
    column_ids = jnp.arange(2 * PANEL, dtype=jnp.int32)
    owners = jnp.take(owner_map, column_ids % devices)
    gathered_ids = (
        (owners % grid_cols) * grid_rows + owners // grid_cols
    ) * (2 * per_device) + column_ids // devices
    pair_ids = jnp.concatenate([gathered_ids, gathered_ids + per_device])
    ordered = jnp.take(raw_images, pair_ids, axis=2)
    feature_rows = ordered.shape[1]
    images = ordered.reshape(2 * feature_rows, 4 * PANEL)
    images = images.reshape(2, feature_rows, 4 * PANEL).transpose(1, 0, 2)
    images = images.reshape(feature_rows, 8 * PANEL).astype(jnp.bfloat16)
    piece = gather_all(images)
    left_prod = jnp.dot(left_vecs, piece, preferred_element_type=jnp.float32)
    right_prod = jnp.dot(right_vecs, piece, preferred_element_type=jnp.float32)
    schur = combine(left_prod, right_prod)
    panel_prod = jnp.dot(gathered_pairs, piece, preferred_element_type=jnp.float32)
    panel_prod = panel_prod.reshape(devices, 2, per_device, 8 * PANEL)
    panel_block = combine(
        panel_prod[:, 0].reshape(devices * per_device, 8 * PANEL),
        panel_prod[:, 1].reshape(devices * per_device, 8 * PANEL),
    )[:, :PANEL]
    order_ids = (gathered_ids // (2 * per_device)) * per_device + gathered_ids % (2 * per_device)
    panel_block = jnp.take(panel_block, order_ids, axis=0)
    chol = jnp.linalg.cholesky(panel_block[:PANEL])
    inverse = lax.linalg.triangular_solve(
        chol, jnp.eye(PANEL, dtype=jnp.float32), left_side=True, lower=True
    )
    ahead = jnp.dot(
        panel_block[PANEL:],
        inverse.T,
        precision=lax.Precision.HIGHEST,
        preferred_element_type=jnp.float32,
    )
    slots = schur.shape[0]
    schur_ids = jnp.arange(slots, dtype=jnp.int32) * devices + residue
    full = jnp.dot(
        schur[:, :PANEL],
        inverse.T,
        precision=lax.Precision.HIGHEST,
        preferred_element_type=jnp.float32,
    )
    full = jnp.where((schur_ids >= start)[:, None], full, jnp.float32(0.0))
    update = schur[:, PANEL:] - jnp.dot(
        full, ahead.T, precision=lax.Precision.HIGHEST, preferred_element_type=jnp.float32
    )
    update = jnp.where((schur_ids >= start + PANEL)[:, None], update, jnp.float32(0.0))
    return relay_rows(full, update, owner_map, devices, grid_rows)


def solution(mesh):
    return jax.shard_map(
        body,
        mesh=mesh,
        in_specs=(
            P(("prow", "pcol"), None),
            P(("prow", "pcol"), None),
            P(("prow", "pcol"), None),
            P(("prow", "pcol"), None),
            P(),
            P(),
        ),
        out_specs=(P("pcol", "prow"), P("pcol", "prow")),
        check_vma=False,
    )
```

```python
import jax
import jax.numpy as jnp
from jax import lax
from jax.sharding import PartitionSpec as P

PANEL = 256


def combine(left_prod, right_prod):
    seg = left_prod.shape[1] // 4
    return (
        left_prod[:, seg : 2 * seg] * right_prod[:, 2 * seg : 3 * seg]
        + right_prod[:, seg : 2 * seg] * left_prod[:, 2 * seg : 3 * seg]
        + left_prod[:, 0:seg] * right_prod[:, 3 * seg : 4 * seg]
        + right_prod[:, 0:seg] * left_prod[:, 3 * seg : 4 * seg]
    )


def gather_prow(x, axis=0):
    size = lax.axis_size("prow")
    me = lax.axis_index("prow")
    step = 1
    while step < size:
        got = lax.ppermute(x, "prow", perm=[(i, i ^ step) for i in range(size)])
        low = (me & step) == 0
        x = jnp.where(
            low, jnp.concatenate([x, got], axis=axis), jnp.concatenate([got, x], axis=axis)
        )
        step *= 2
    return x


def gather_all(x):
    return lax.all_gather(gather_prow(x), "pcol", axis=0, tiled=True)


def relay_rows(first_part, second_part, owner_map, devices, grid_rows):
    slots = first_part.shape[0]
    height = PANEL // devices
    groups = slots // (grid_rows * height)
    grid_cols = devices // grid_rows
    narrow = PANEL // grid_cols
    stacked = jnp.stack([first_part, second_part], axis=1)
    stacked = stacked.reshape(groups, grid_rows, height, 2, grid_cols, narrow)
    outgoing = stacked.transpose(1, 4, 3, 5, 0, 2).reshape(devices, 2 * narrow * groups * height)
    arrived = lax.all_to_all(outgoing, ("prow", "pcol"), split_axis=0, concat_axis=0, tiled=True)
    ordered = jnp.take(arrived, owner_map, axis=0)
    ordered = ordered.reshape(devices, 2, narrow, groups, height)
    placed = ordered.transpose(1, 2, 3, 4, 0).reshape(2, narrow, groups * height * devices)
    return (placed[0], placed[1])


def body(left_vecs, right_vecs, primal, dual_inverse, owner_map, panel_index):
    devices = lax.axis_size(("prow", "pcol"))
    grid_rows = lax.axis_size("prow")
    grid_cols = lax.axis_size("pcol")
    per_device = 2 * PANEL // devices
    start = panel_index[0] * PANEL
    first_slot = start // devices
    me = lax.axis_index("prow") * grid_cols + lax.axis_index("pcol")
    residue = jnp.sum(jnp.where(owner_map == me, jnp.arange(devices, dtype=jnp.int32), 0))
    panel_left = lax.dynamic_slice_in_dim(left_vecs, first_slot, per_device, 0)
    panel_right = lax.dynamic_slice_in_dim(right_vecs, first_slot, per_device, 0)
    panel_pairs = jnp.concatenate([panel_left, panel_right], axis=0)
    moves = [
        ((q * grid_rows + p), (p * grid_cols + q))
        for p in range(grid_rows)
        for q in range(grid_cols)
    ]
    matrices = lax.ppermute(
        jnp.stack([primal, dual_inverse], axis=0), ("prow", "pcol"), perm=moves
    )
    matrices = gather_prow(matrices, axis=1)
    gathered_pairs = gather_all(panel_pairs)
    raw_images = jnp.einsum(
        "gfn,mn->gfm", matrices, gathered_pairs, preferred_element_type=jnp.float32
    )
    column_ids = jnp.arange(2 * PANEL, dtype=jnp.int32)
    owners = jnp.take(owner_map, column_ids % devices)
    gathered_ids = (
        (owners % grid_cols) * grid_rows + owners // grid_cols
    ) * (2 * per_device) + column_ids // devices
    feature_rows = raw_images.shape[1]

    def image_half(h):
        ids = gathered_ids[h * PANEL : (h + 1) * PANEL]
        ordered = jnp.take(raw_images, jnp.concatenate([ids, ids + per_device]), axis=2)
        ordered = ordered.transpose(1, 0, 2).reshape(feature_rows, 4 * PANEL)
        return lax.all_gather(ordered.astype(jnp.bfloat16), "pcol", axis=0, tiled=True)

    piece = image_half(0)
    panel_prod = jnp.dot(gathered_pairs, piece, preferred_element_type=jnp.float32)
    panel_prod = panel_prod.reshape(devices, 2, per_device, 4 * PANEL)
    panel_block = combine(
        panel_prod[:, 0].reshape(devices * per_device, 4 * PANEL),
        panel_prod[:, 1].reshape(devices * per_device, 4 * PANEL),
    )
    schur_first = combine(
        jnp.dot(left_vecs, piece, preferred_element_type=jnp.float32),
        jnp.dot(right_vecs, piece, preferred_element_type=jnp.float32),
    )
    piece = image_half(1)
    schur_second = combine(
        jnp.dot(left_vecs, piece, preferred_element_type=jnp.float32),
        jnp.dot(right_vecs, piece, preferred_element_type=jnp.float32),
    )
    order_ids = (gathered_ids // (2 * per_device)) * per_device + gathered_ids % (2 * per_device)
    panel_block = jnp.take(panel_block, order_ids, axis=0)
    chol = jnp.linalg.cholesky(panel_block[:PANEL])
    inverse = lax.linalg.triangular_solve(
        chol, jnp.eye(PANEL, dtype=jnp.float32), left_side=True, lower=True
    )
    ahead = jnp.dot(
        panel_block[PANEL:],
        inverse.T,
        precision=lax.Precision.HIGHEST,
        preferred_element_type=jnp.float32,
    )
    slots = schur_first.shape[0]
    schur_ids = jnp.arange(slots, dtype=jnp.int32) * devices + residue
    full = jnp.dot(
        schur_first,
        inverse.T,
        precision=lax.Precision.HIGHEST,
        preferred_element_type=jnp.float32,
    )
    full = jnp.where((schur_ids >= start)[:, None], full, jnp.float32(0.0))
    update = schur_second - jnp.dot(
        full, ahead.T, precision=lax.Precision.HIGHEST, preferred_element_type=jnp.float32
    )
    update = jnp.where((schur_ids >= start + PANEL)[:, None], update, jnp.float32(0.0))
    return relay_rows(full, update, owner_map, devices, grid_rows)


def solution(mesh):
    return jax.shard_map(
        body,
        mesh=mesh,
        in_specs=(
            P(("prow", "pcol"), None),
            P(("prow", "pcol"), None),
            P(("prow", "pcol"), None),
            P(("prow", "pcol"), None),
            P(),
            P(),
        ),
        out_specs=(P("pcol", "prow"), P("pcol", "prow")),
        check_vma=False,
    )
```

```python
import jax
import jax.numpy as jnp
from jax import lax
from jax.sharding import PartitionSpec as P

PANEL = 256


def combine(left_prod, right_prod):
    seg = left_prod.shape[1] // 4
    return (
        left_prod[:, seg : 2 * seg] * right_prod[:, 2 * seg : 3 * seg]
        + right_prod[:, seg : 2 * seg] * left_prod[:, 2 * seg : 3 * seg]
        + left_prod[:, 0:seg] * right_prod[:, 3 * seg : 4 * seg]
        + right_prod[:, 0:seg] * left_prod[:, 3 * seg : 4 * seg]
    )


def gather_prow(x, axis=0):
    size = lax.axis_size("prow")
    me = lax.axis_index("prow")
    step = 1
    while step < size:
        got = lax.ppermute(x, "prow", perm=[(i, i ^ step) for i in range(size)])
        low = (me & step) == 0
        x = jnp.where(
            low, jnp.concatenate([x, got], axis=axis), jnp.concatenate([got, x], axis=axis)
        )
        step *= 2
    return x


def gather_all(x):
    return lax.all_gather(gather_prow(x), "pcol", axis=0, tiled=True)


def relay_rows(full_t, update_t, owner_map, devices, grid_rows):
    cols, slots = full_t.shape
    grid_cols = devices // grid_rows
    per_row = slots // grid_rows
    both = jnp.stack(
        [full_t.reshape(cols, grid_rows, per_row), update_t.reshape(cols, grid_rows, per_row)],
        axis=2,
    ).reshape(cols, grid_rows, 2 * per_row)
    outgoing = both.transpose(1, 0, 2).reshape(devices, cols // grid_cols * 2 * per_row)
    arrived = lax.all_to_all(outgoing, ("prow", "pcol"), split_axis=0, concat_axis=0, tiled=True)
    ordered = jnp.take(arrived, owner_map, axis=0).T
    narrow = cols // grid_cols
    placed = ordered.reshape(narrow, 2, per_row * devices).transpose(1, 0, 2)
    return (placed[0], placed[1])


def body(left_vecs, right_vecs, primal, dual_inverse, owner_map, panel_index):
    devices = lax.axis_size(("prow", "pcol"))
    grid_rows = lax.axis_size("prow")
    grid_cols = lax.axis_size("pcol")
    per_device = 2 * PANEL // devices
    start = panel_index[0] * PANEL
    first_slot = start // devices
    me = lax.axis_index("prow") * grid_cols + lax.axis_index("pcol")
    residue = jnp.sum(jnp.where(owner_map == me, jnp.arange(devices, dtype=jnp.int32), 0))
    panel_left = lax.dynamic_slice_in_dim(left_vecs, first_slot, per_device, 0)
    panel_right = lax.dynamic_slice_in_dim(right_vecs, first_slot, per_device, 0)
    panel_pairs = jnp.concatenate([panel_left, panel_right], axis=0)
    moves = [
        ((q * grid_rows + p), (p * grid_cols + q))
        for p in range(grid_rows)
        for q in range(grid_cols)
    ]
    matrices = lax.ppermute(
        jnp.stack([primal, dual_inverse], axis=0), ("prow", "pcol"), perm=moves
    )
    gathered_pairs = gather_all(panel_pairs)
    raw_images = jnp.einsum(
        "gfn,mn->gfm", matrices, gathered_pairs, preferred_element_type=jnp.float32
    )
    column_ids = jnp.arange(2 * PANEL, dtype=jnp.int32)
    owners = jnp.take(owner_map, column_ids % devices)
    gathered_ids = (
        (owners % grid_cols) * grid_rows + owners // grid_cols
    ) * (2 * per_device) + column_ids // devices
    pair_ids = jnp.concatenate([gathered_ids, gathered_ids + per_device])
    ordered = jnp.take(raw_images, pair_ids, axis=2)
    feature_rows = ordered.shape[1]
    images = ordered.transpose(1, 0, 2).reshape(feature_rows, 8 * PANEL).astype(jnp.bfloat16)
    images = gather_prow(images)
    prow_rows = images.shape[0]
    images = images.reshape(prow_rows, 4, 2, PANEL)

    def image_half(h):
        part = images[:, :, h, :].reshape(prow_rows, 4 * PANEL)
        return lax.all_gather(part, "pcol", axis=0, tiled=True)

    slots = left_vecs.shape[0]
    height = PANEL // devices
    blocks = slots // (grid_rows * height)

    def slot_order(x):
        x = x.reshape(blocks, grid_rows, height, x.shape[1]).transpose(1, 0, 2, 3)
        return x.reshape(slots, x.shape[3])

    piece = image_half(0)
    panel_vecs = jnp.take(gathered_pairs, pair_ids, axis=0)
    panel_block = combine(
        jnp.dot(panel_vecs[: 2 * PANEL], piece, preferred_element_type=jnp.float32),
        jnp.dot(panel_vecs[2 * PANEL :], piece, preferred_element_type=jnp.float32),
    )
    schur_first = slot_order(
        combine(
            jnp.dot(left_vecs, piece, preferred_element_type=jnp.float32),
            jnp.dot(right_vecs, piece, preferred_element_type=jnp.float32),
        )
    )
    piece = image_half(1)
    schur_second = slot_order(
        combine(
            jnp.dot(left_vecs, piece, preferred_element_type=jnp.float32),
            jnp.dot(right_vecs, piece, preferred_element_type=jnp.float32),
        )
    )
    chol = jnp.linalg.cholesky(panel_block[:PANEL])
    inverse = lax.linalg.triangular_solve(
        chol, jnp.eye(PANEL, dtype=jnp.float32), left_side=True, lower=True
    )
    ahead = jnp.dot(
        panel_block[PANEL:],
        inverse.T,
        precision=lax.Precision.HIGHEST,
        preferred_element_type=jnp.float32,
    )
    place = jnp.arange(slots, dtype=jnp.int32)
    slot_of = (place % (blocks * height)) // height * (grid_rows * height) + (
        place // (blocks * height)
    ) * height + place % height
    schur_ids = slot_of * devices + residue
    full_t = lax.dot_general(
        inverse,
        schur_first,
        (((1,), (1,)), ((), ())),
        precision=lax.Precision.HIGHEST,
        preferred_element_type=jnp.float32,
    )
    full_t = jnp.where((schur_ids >= start)[None, :], full_t, jnp.float32(0.0))
    update_t = schur_second.T - jnp.dot(
        ahead, full_t, precision=lax.Precision.HIGHEST, preferred_element_type=jnp.float32
    )
    update_t = jnp.where((schur_ids >= start + PANEL)[None, :], update_t, jnp.float32(0.0))
    return relay_rows(full_t, update_t, owner_map, devices, grid_rows)


def solution(mesh):
    return jax.shard_map(
        body,
        mesh=mesh,
        in_specs=(
            P(("prow", "pcol"), None),
            P(("prow", "pcol"), None),
            P(("prow", "pcol"), None),
            P(("prow", "pcol"), None),
            P(),
            P(),
        ),
        out_specs=(P("pcol", "prow"), P("pcol", "prow")),
        check_vma=False,
    )
```

```python
import jax
import jax.numpy as jnp
from jax import lax
from jax.sharding import PartitionSpec as P


PANEL = 256


def combine(left_prod, right_prod):
    seg = left_prod.shape[1] // 4
    return (
        left_prod[:, seg : 2 * seg] * right_prod[:, 2 * seg : 3 * seg]
        + right_prod[:, seg : 2 * seg] * left_prod[:, 2 * seg : 3 * seg]
        + left_prod[:, 0:seg] * right_prod[:, 3 * seg : 4 * seg]
        + right_prod[:, 0:seg] * left_prod[:, 3 * seg : 4 * seg]
    )


def gather_prow(x, axis=0):
    size = lax.axis_size("prow")
    me = lax.axis_index("prow")
    step = 1
    while step < size:
        got = lax.ppermute(x, "prow", perm=[(i, i ^ step) for i in range(size)])
        low = (me & step) == 0
        x = jnp.where(
            low, jnp.concatenate([x, got], axis=axis), jnp.concatenate([got, x], axis=axis)
        )
        step *= 2
    return x


def gather_all(x):
    return lax.all_gather(gather_prow(x), "pcol", axis=0, tiled=True)


def relay_rows(full_t, update_t, owner_map, devices, grid_rows):
    cols, slots = full_t.shape
    grid_cols = devices // grid_rows
    per_row = slots // grid_rows
    both = jnp.stack(
        [full_t.reshape(cols, grid_rows, per_row), update_t.reshape(cols, grid_rows, per_row)],
        axis=2,
    ).reshape(cols, grid_rows, 2 * per_row)
    outgoing = both.transpose(1, 0, 2).reshape(devices, cols // grid_cols * 2 * per_row)
    arrived = lax.all_to_all(outgoing, ("prow", "pcol"), split_axis=0, concat_axis=0, tiled=True)
    ordered = jnp.take(arrived, owner_map, axis=0).T
    narrow = cols // grid_cols
    placed = ordered.reshape(narrow, 2, per_row * devices).transpose(1, 0, 2)
    return (placed[0], placed[1])


def body(left_vecs, right_vecs, primal, dual_inverse, owner_map, panel_index):
    devices = lax.axis_size(("prow", "pcol"))
    grid_rows = lax.axis_size("prow")
    grid_cols = lax.axis_size("pcol")
    per_device = 2 * PANEL // devices
    start = panel_index[0] * PANEL
    first_slot = start // devices
    me = lax.axis_index("prow") * grid_cols + lax.axis_index("pcol")
    residue = jnp.sum(jnp.where(owner_map == me, jnp.arange(devices, dtype=jnp.int32), 0))
    moves = [
        ((q * grid_rows + p), (p * grid_cols + q))
        for p in range(grid_rows)
        for q in range(grid_cols)
    ]
    matrices = lax.ppermute(
        jnp.stack([primal, dual_inverse], axis=0), ("prow", "pcol"), perm=moves
    )
    half_slots = per_device // 2
    column_ids = jnp.arange(PANEL, dtype=jnp.int32)
    owners = jnp.take(owner_map, column_ids % devices)
    gathered_ids = (
        (owners % grid_cols) * grid_rows + owners // grid_cols
    ) * (2 * half_slots) + column_ids // devices
    pair_ids = jnp.concatenate([gathered_ids, gathered_ids + half_slots])
    later = jnp.take(owner_map, (column_ids + PANEL) % devices)
    later_ids = (
        (later % grid_cols) * grid_rows + later // grid_cols
    ) * (2 * half_slots) + column_ids // devices
    later_ids = jnp.concatenate([later_ids, later_ids + half_slots])

    def panel_half(h):
        first = first_slot + h * half_slots
        rows = jnp.concatenate(
            [
                lax.dynamic_slice_in_dim(left_vecs, first, half_slots, 0),
                lax.dynamic_slice_in_dim(right_vecs, first, half_slots, 0),
            ],
            axis=0,
        )
        return gather_all(rows)

    def image_half(gathered, ids):
        raw = jnp.einsum("gfn,mn->gfm", matrices, gathered, preferred_element_type=jnp.float32)
        ordered = jnp.take(raw, ids, axis=2)
        feature_rows = ordered.shape[1]
        part = ordered.transpose(1, 0, 2).reshape(feature_rows, 4 * PANEL).astype(jnp.bfloat16)
        part = gather_prow(part)
        return lax.all_gather(part, "pcol", axis=0, tiled=True)

    slots = left_vecs.shape[0]
    height = PANEL // devices
    blocks = slots // (grid_rows * height)

    def slot_order(x):
        x = x.reshape(blocks, grid_rows, height, x.shape[1]).transpose(1, 0, 2, 3)
        return x.reshape(slots, x.shape[3])

    def panel_rows(gathered, piece):
        vecs = jnp.take(gathered, pair_ids, axis=0)
        return combine(
            jnp.dot(vecs[:PANEL], piece, preferred_element_type=jnp.float32),
            jnp.dot(vecs[PANEL:], piece, preferred_element_type=jnp.float32),
        )

    gathered_first = panel_half(0)
    gathered_second = panel_half(1)
    piece = image_half(gathered_first, pair_ids)
    panel_top = panel_rows(gathered_first, piece)
    panel_bottom = panel_rows(gathered_second, piece)
    schur_first = slot_order(
        combine(
            jnp.dot(left_vecs, piece, preferred_element_type=jnp.float32),
            jnp.dot(right_vecs, piece, preferred_element_type=jnp.float32),
        )
    )
    piece = image_half(gathered_second, later_ids)
    schur_second = slot_order(
        combine(
            jnp.dot(left_vecs, piece, preferred_element_type=jnp.float32),
            jnp.dot(right_vecs, piece, preferred_element_type=jnp.float32),
        )
    )
    chol = jnp.linalg.cholesky(panel_top)
    inverse = lax.linalg.triangular_solve(
        chol, jnp.eye(PANEL, dtype=jnp.float32), left_side=True, lower=True
    )
    ahead = jnp.dot(
        panel_bottom,
        inverse.T,
        precision=lax.Precision.HIGHEST,
        preferred_element_type=jnp.float32,
    )
    place = jnp.arange(slots, dtype=jnp.int32)
    slot_of = (place % (blocks * height)) // height * (grid_rows * height) + (
        place // (blocks * height)
    ) * height + place % height
    schur_ids = slot_of * devices + residue
    full_t = lax.dot_general(
        inverse,
        schur_first,
        (((1,), (1,)), ((), ())),
        precision=lax.Precision.HIGHEST,
        preferred_element_type=jnp.float32,
    )
    full_t = jnp.where((schur_ids >= start)[None, :], full_t, jnp.float32(0.0))
    update_t = schur_second.T - jnp.dot(
        ahead, full_t, precision=lax.Precision.HIGHEST, preferred_element_type=jnp.float32
    )
    update_t = jnp.where((schur_ids >= start + PANEL)[None, :], update_t, jnp.float32(0.0))
    return relay_rows(full_t, update_t, owner_map, devices, grid_rows)


def solution(mesh):
    return jax.shard_map(
        body,
        mesh=mesh,
        in_specs=(
            P(("prow", "pcol"), None),
            P(("prow", "pcol"), None),
            P(("prow", "pcol"), None),
            P(("prow", "pcol"), None),
            P(),
            P(),
        ),
        out_specs=(P("pcol", "prow"), P("pcol", "prow")),
        check_vma=False,
    )
```

```python
import jax
import jax.numpy as jnp
from jax import lax
from jax.sharding import PartitionSpec as P


PANEL = 256


def combine(left_prod, right_prod):
    seg = left_prod.shape[1] // 4
    return (
        left_prod[:, seg : 2 * seg] * right_prod[:, 2 * seg : 3 * seg]
        + right_prod[:, seg : 2 * seg] * left_prod[:, 2 * seg : 3 * seg]
        + left_prod[:, 0:seg] * right_prod[:, 3 * seg : 4 * seg]
        + right_prod[:, 0:seg] * left_prod[:, 3 * seg : 4 * seg]
    )


def gather_prow(x, axis=0):
    size = lax.axis_size("prow")
    me = lax.axis_index("prow")
    step = 1
    while step < size:
        got = lax.ppermute(x, "prow", perm=[(i, i ^ step) for i in range(size)])
        low = (me & step) == 0
        x = jnp.where(
            low, jnp.concatenate([x, got], axis=axis), jnp.concatenate([got, x], axis=axis)
        )
        step *= 2
    return x


def gather_all(x):
    return lax.all_gather(gather_prow(x), "pcol", axis=0, tiled=True)


def relay_rows(full_t, update_t, owner_map, devices, grid_rows):
    cols, slots = full_t.shape
    grid_cols = devices // grid_rows
    per_row = slots // grid_rows
    both = jnp.stack(
        [full_t.reshape(cols, grid_rows, per_row), update_t.reshape(cols, grid_rows, per_row)],
        axis=2,
    ).reshape(cols, grid_rows, 2 * per_row)
    outgoing = both.transpose(1, 0, 2).reshape(devices, cols // grid_cols * 2 * per_row)
    arrived = lax.all_to_all(outgoing, ("prow", "pcol"), split_axis=0, concat_axis=0, tiled=True)
    ordered = jnp.take(arrived, owner_map, axis=0).T
    narrow = cols // grid_cols
    placed = ordered.reshape(narrow, 2, per_row * devices).transpose(1, 0, 2)
    return (placed[0], placed[1])


def body(left_vecs, right_vecs, primal, dual_inverse, owner_map, panel_index):
    devices = lax.axis_size(("prow", "pcol"))
    grid_rows = lax.axis_size("prow")
    grid_cols = lax.axis_size("pcol")
    per_device = 2 * PANEL // devices
    start = panel_index[0] * PANEL
    first_slot = start // devices
    me = lax.axis_index("prow") * grid_cols + lax.axis_index("pcol")
    residue = jnp.sum(jnp.where(owner_map == me, jnp.arange(devices, dtype=jnp.int32), 0))
    moves = [
        ((q * grid_rows + p), (p * grid_cols + q))
        for p in range(grid_rows)
        for q in range(grid_cols)
    ]
    matrices = lax.ppermute(
        jnp.stack([primal, dual_inverse], axis=0), ("prow", "pcol"), perm=moves
    )
    copies = jnp.broadcast_to(matrices[None], (grid_rows,) + matrices.shape)
    copies = lax.all_to_all(copies, "prow", split_axis=0, concat_axis=0, tiled=True)
    matrices = copies.transpose(1, 0, 2, 3).reshape(2, grid_rows * matrices.shape[1], -1)
    column_ids = jnp.arange(2 * PANEL, dtype=jnp.int32)
    owners = jnp.take(owner_map, column_ids % devices)
    gathered_ids = (
        (owners % grid_cols) * grid_rows + owners // grid_cols
    ) * (2 * per_device) + column_ids // devices
    pair_ids = jnp.concatenate([gathered_ids, gathered_ids + per_device])
    panel_pairs = jnp.concatenate(
        [
            lax.dynamic_slice_in_dim(left_vecs, first_slot, per_device, 0),
            lax.dynamic_slice_in_dim(right_vecs, first_slot, per_device, 0),
        ],
        axis=0,
    )
    gathered_pairs = gather_all(panel_pairs)
    raw_images = jnp.einsum(
        "gfn,mn->gfm", matrices, gathered_pairs, preferred_element_type=jnp.float32
    )
    feature_rows = raw_images.shape[1]

    def image_half(h):
        ids = gathered_ids[h * PANEL : (h + 1) * PANEL]
        ordered = jnp.take(raw_images, jnp.concatenate([ids, ids + per_device]), axis=2)
        part = ordered.transpose(1, 0, 2).reshape(feature_rows, 4 * PANEL).astype(jnp.bfloat16)
        return lax.all_gather(part, "pcol", axis=0, tiled=True)

    slots = left_vecs.shape[0]
    height = PANEL // devices
    blocks = slots // (grid_rows * height)

    def slot_order(x):
        x = x.reshape(blocks, grid_rows, height, x.shape[1]).transpose(1, 0, 2, 3)
        return x.reshape(slots, x.shape[3])

    piece = image_half(0)
    panel_vecs = jnp.take(gathered_pairs, pair_ids, axis=0)
    panel_block = combine(
        jnp.dot(panel_vecs[: 2 * PANEL], piece, preferred_element_type=jnp.float32),
        jnp.dot(panel_vecs[2 * PANEL :], piece, preferred_element_type=jnp.float32),
    )
    panel_top = panel_block[:PANEL]
    panel_bottom = panel_block[PANEL:]
    schur_first = slot_order(
        combine(
            jnp.dot(left_vecs, piece, preferred_element_type=jnp.float32),
            jnp.dot(right_vecs, piece, preferred_element_type=jnp.float32),
        )
    )
    piece = image_half(1)
    schur_second = slot_order(
        combine(
            jnp.dot(left_vecs, piece, preferred_element_type=jnp.float32),
            jnp.dot(right_vecs, piece, preferred_element_type=jnp.float32),
        )
    )
    chol = jnp.linalg.cholesky(panel_top)
    inverse = lax.linalg.triangular_solve(
        chol, jnp.eye(PANEL, dtype=jnp.float32), left_side=True, lower=True
    )
    ahead = jnp.dot(
        panel_bottom,
        inverse.T,
        precision=lax.Precision.HIGHEST,
        preferred_element_type=jnp.float32,
    )
    place = jnp.arange(slots, dtype=jnp.int32)
    slot_of = (place % (blocks * height)) // height * (grid_rows * height) + (
        place // (blocks * height)
    ) * height + place % height
    schur_ids = slot_of * devices + residue
    full_t = lax.dot_general(
        inverse,
        schur_first,
        (((1,), (1,)), ((), ())),
        precision=lax.Precision.HIGHEST,
        preferred_element_type=jnp.float32,
    )
    full_t = jnp.where((schur_ids >= start)[None, :], full_t, jnp.float32(0.0))
    update_t = schur_second.T - jnp.dot(
        ahead, full_t, precision=lax.Precision.HIGHEST, preferred_element_type=jnp.float32
    )
    update_t = jnp.where((schur_ids >= start + PANEL)[None, :], update_t, jnp.float32(0.0))
    return relay_rows(full_t, update_t, owner_map, devices, grid_rows)


def solution(mesh):
    return jax.shard_map(
        body,
        mesh=mesh,
        in_specs=(
            P(("prow", "pcol"), None),
            P(("prow", "pcol"), None),
            P(("prow", "pcol"), None),
            P(("prow", "pcol"), None),
            P(),
            P(),
        ),
        out_specs=(P("pcol", "prow"), P("pcol", "prow")),
        check_vma=False,
    )
```

```python
import jax
import jax.numpy as jnp
from jax import lax
from jax.sharding import PartitionSpec as P


PANEL = 256


def combine(left_prod, right_prod):
    seg = left_prod.shape[1] // 4
    return (
        left_prod[:, seg : 2 * seg] * right_prod[:, 2 * seg : 3 * seg]
        + right_prod[:, seg : 2 * seg] * left_prod[:, 2 * seg : 3 * seg]
        + left_prod[:, 0:seg] * right_prod[:, 3 * seg : 4 * seg]
        + right_prod[:, 0:seg] * left_prod[:, 3 * seg : 4 * seg]
    )


def gather_prow(x, axis=0):
    size = lax.axis_size("prow")
    me = lax.axis_index("prow")
    step = 1
    while step < size:
        got = lax.ppermute(x, "prow", perm=[(i, i ^ step) for i in range(size)])
        low = (me & step) == 0
        x = jnp.where(
            low, jnp.concatenate([x, got], axis=axis), jnp.concatenate([got, x], axis=axis)
        )
        step *= 2
    return x


def gather_all(x):
    return lax.all_gather(gather_prow(x), "pcol", axis=0, tiled=True)


def mm(a, b):
    return jnp.dot(a, b, precision=lax.Precision.HIGHEST, preferred_element_type=jnp.float32)


def block_inverse_factor(base):
    half = base.shape[0] // 2
    eye = jnp.eye(half, dtype=jnp.float32)
    sym = (base + base.T) * jnp.float32(0.5)
    first = jnp.linalg.cholesky(sym[:half, :half], symmetrize_input=False)
    first_inv = lax.linalg.triangular_solve(first, eye, left_side=True, lower=True)
    lower = mm(sym[half:, :half], first_inv.T)
    second = jnp.linalg.cholesky(sym[half:, half:] - mm(lower, lower.T), symmetrize_input=False)
    second_inv = lax.linalg.triangular_solve(second, eye, left_side=True, lower=True)
    corner = -mm(second_inv, mm(lower, first_inv))
    top = jnp.concatenate([first_inv, jnp.zeros_like(first_inv)], axis=1)
    return jnp.concatenate([top, jnp.concatenate([corner, second_inv], axis=1)], axis=0)


def relay_rows(full_t, update_t, owner_map, devices, grid_rows):
    cols, slots = full_t.shape
    grid_cols = devices // grid_rows
    per_row = slots // grid_rows
    both = jnp.stack(
        [full_t.reshape(cols, grid_rows, per_row), update_t.reshape(cols, grid_rows, per_row)],
        axis=2,
    ).reshape(cols, grid_rows, 2 * per_row)
    outgoing = both.transpose(1, 0, 2).reshape(devices, cols // grid_cols * 2 * per_row)
    arrived = lax.all_to_all(outgoing, ("prow", "pcol"), split_axis=0, concat_axis=0, tiled=True)
    ordered = jnp.take(arrived, owner_map, axis=0).T
    narrow = cols // grid_cols
    placed = ordered.reshape(narrow, 2, per_row * devices).transpose(1, 0, 2)
    return (placed[0], placed[1])


def body(left_vecs, right_vecs, primal, dual_inverse, owner_map, panel_index):
    devices = lax.axis_size(("prow", "pcol"))
    grid_rows = lax.axis_size("prow")
    grid_cols = lax.axis_size("pcol")
    per_device = 2 * PANEL // devices
    start = panel_index[0] * PANEL
    first_slot = start // devices
    me = lax.axis_index("prow") * grid_cols + lax.axis_index("pcol")
    residue = jnp.sum(jnp.where(owner_map == me, jnp.arange(devices, dtype=jnp.int32), 0))
    moves = [
        ((q * grid_rows + p), (p * grid_cols + q))
        for p in range(grid_rows)
        for q in range(grid_cols)
    ]
    matrices = lax.ppermute(
        jnp.stack([primal, dual_inverse], axis=0), ("prow", "pcol"), perm=moves
    )
    half_slots = per_device // 2
    column_ids = jnp.arange(PANEL, dtype=jnp.int32)
    owners = jnp.take(owner_map, column_ids % devices)
    gathered_ids = (
        (owners % grid_cols) * grid_rows + owners // grid_cols
    ) * (2 * half_slots) + column_ids // devices
    pair_ids = jnp.concatenate([gathered_ids, gathered_ids + half_slots])
    later = jnp.take(owner_map, (column_ids + PANEL) % devices)
    later_ids = (
        (later % grid_cols) * grid_rows + later // grid_cols
    ) * (2 * half_slots) + column_ids // devices
    later_ids = jnp.concatenate([later_ids, later_ids + half_slots])

    def panel_half(h):
        first = first_slot + h * half_slots
        rows = jnp.concatenate(
            [
                lax.dynamic_slice_in_dim(left_vecs, first, half_slots, 0),
                lax.dynamic_slice_in_dim(right_vecs, first, half_slots, 0),
            ],
            axis=0,
        )
        return gather_all(rows)

    def image_half(gathered, ids):
        raw = jnp.einsum("gfn,mn->gfm", matrices, gathered, preferred_element_type=jnp.float32)
        ordered = jnp.take(raw, ids, axis=2)
        feature_rows = ordered.shape[1]
        part = ordered.transpose(1, 0, 2).reshape(feature_rows, 4 * PANEL).astype(jnp.bfloat16)
        part = gather_prow(part)
        return lax.all_gather(part, "pcol", axis=0, tiled=True)

    slots = left_vecs.shape[0]
    height = PANEL // devices
    blocks = slots // (grid_rows * height)

    def slot_order(x):
        x = x.reshape(blocks, grid_rows, height, x.shape[1]).transpose(1, 0, 2, 3)
        return x.reshape(slots, x.shape[3])

    def panel_rows(gathered, piece):
        vecs = jnp.take(gathered, pair_ids, axis=0)
        return combine(
            jnp.dot(vecs[:PANEL], piece, preferred_element_type=jnp.float32),
            jnp.dot(vecs[PANEL:], piece, preferred_element_type=jnp.float32),
        )

    gathered_first = panel_half(0)
    gathered_second = panel_half(1)
    piece = image_half(gathered_first, pair_ids)
    panel_top = panel_rows(gathered_first, piece)
    panel_bottom = panel_rows(gathered_second, piece)
    schur_first = slot_order(
        combine(
            jnp.dot(left_vecs, piece, preferred_element_type=jnp.float32),
            jnp.dot(right_vecs, piece, preferred_element_type=jnp.float32),
        )
    )
    piece = image_half(gathered_second, later_ids)
    schur_second = slot_order(
        combine(
            jnp.dot(left_vecs, piece, preferred_element_type=jnp.float32),
            jnp.dot(right_vecs, piece, preferred_element_type=jnp.float32),
        )
    )
    inverse = block_inverse_factor(panel_top)
    ahead = jnp.dot(
        panel_bottom,
        inverse.T,
        precision=lax.Precision.HIGHEST,
        preferred_element_type=jnp.float32,
    )
    place = jnp.arange(slots, dtype=jnp.int32)
    slot_of = (place % (blocks * height)) // height * (grid_rows * height) + (
        place // (blocks * height)
    ) * height + place % height
    schur_ids = slot_of * devices + residue
    full_t = lax.dot_general(
        inverse,
        schur_first,
        (((1,), (1,)), ((), ())),
        precision=lax.Precision.HIGHEST,
        preferred_element_type=jnp.float32,
    )
    full_t = jnp.where((schur_ids >= start)[None, :], full_t, jnp.float32(0.0))
    update_t = schur_second.T - jnp.dot(
        ahead, full_t, precision=lax.Precision.HIGHEST, preferred_element_type=jnp.float32
    )
    update_t = jnp.where((schur_ids >= start + PANEL)[None, :], update_t, jnp.float32(0.0))
    return relay_rows(full_t, update_t, owner_map, devices, grid_rows)


def solution(mesh):
    return jax.shard_map(
        body,
        mesh=mesh,
        in_specs=(
            P(("prow", "pcol"), None),
            P(("prow", "pcol"), None),
            P(("prow", "pcol"), None),
            P(("prow", "pcol"), None),
            P(),
            P(),
        ),
        out_specs=(P("pcol", "prow"), P("pcol", "prow")),
        check_vma=False,
    )
```

```python
import jax
import jax.numpy as jnp
from jax import lax
from jax.sharding import PartitionSpec as P


PANEL = 256


def combine(left_prod, right_prod):
    seg = left_prod.shape[1] // 4
    return (
        left_prod[:, seg : 2 * seg] * right_prod[:, 2 * seg : 3 * seg]
        + right_prod[:, seg : 2 * seg] * left_prod[:, 2 * seg : 3 * seg]
        + left_prod[:, 0:seg] * right_prod[:, 3 * seg : 4 * seg]
        + right_prod[:, 0:seg] * left_prod[:, 3 * seg : 4 * seg]
    )


def gather_prow(x, axis=0):
    size = lax.axis_size("prow")
    me = lax.axis_index("prow")
    step = 1
    while step < size:
        got = lax.ppermute(x, "prow", perm=[(i, i ^ step) for i in range(size)])
        low = (me & step) == 0
        x = jnp.where(
            low, jnp.concatenate([x, got], axis=axis), jnp.concatenate([got, x], axis=axis)
        )
        step *= 2
    return x


def gather_all(x):
    return lax.all_gather(gather_prow(x), "pcol", axis=0, tiled=True)


def mm(a, b):
    return jnp.dot(a, b, precision=lax.Precision.HIGHEST, preferred_element_type=jnp.float32)


def block_inverse_factor(base):
    half = base.shape[0] // 2
    eye = jnp.eye(half, dtype=jnp.float32)
    sym = (base + base.T) * jnp.float32(0.5)
    first = jnp.linalg.cholesky(sym[:half, :half], symmetrize_input=False)
    first_inv = lax.linalg.triangular_solve(first, eye, left_side=True, lower=True)
    lower = mm(sym[half:, :half], first_inv.T)
    second = jnp.linalg.cholesky(sym[half:, half:] - mm(lower, lower.T), symmetrize_input=False)
    second_inv = lax.linalg.triangular_solve(second, eye, left_side=True, lower=True)
    corner = -mm(second_inv, mm(lower, first_inv))
    top = jnp.concatenate([first_inv, jnp.zeros_like(first_inv)], axis=1)
    return jnp.concatenate([top, jnp.concatenate([corner, second_inv], axis=1)], axis=0)


def relay_rows(full_t, update_t, owner_map, devices, grid_rows):
    cols, slots = full_t.shape
    grid_cols = devices // grid_rows
    per_row = slots // grid_rows
    both = jnp.stack(
        [full_t.reshape(cols, grid_rows, per_row), update_t.reshape(cols, grid_rows, per_row)],
        axis=2,
    ).reshape(cols, grid_rows, 2 * per_row)
    outgoing = both.transpose(1, 0, 2).reshape(devices, cols // grid_cols * 2 * per_row)
    arrived = lax.all_to_all(outgoing, ("prow", "pcol"), split_axis=0, concat_axis=0, tiled=True)
    ordered = jnp.take(arrived, owner_map, axis=0).T
    narrow = cols // grid_cols
    placed = ordered.reshape(narrow, 2, per_row * devices).transpose(1, 0, 2)
    return (placed[0], placed[1])


def body(left_vecs, right_vecs, primal, dual_inverse, owner_map, panel_index):
    devices = lax.axis_size(("prow", "pcol"))
    grid_rows = lax.axis_size("prow")
    grid_cols = lax.axis_size("pcol")
    per_device = 2 * PANEL // devices
    start = panel_index[0] * PANEL
    first_slot = start // devices
    me = lax.axis_index("prow") * grid_cols + lax.axis_index("pcol")
    residue = jnp.sum(jnp.where(owner_map == me, jnp.arange(devices, dtype=jnp.int32), 0))
    moves = [
        ((q * grid_rows + p), (p * grid_cols + q))
        for p in range(grid_rows)
        for q in range(grid_cols)
    ]
    matrices = lax.ppermute(
        jnp.stack([primal, dual_inverse], axis=0), ("prow", "pcol"), perm=moves
    )
    half_slots = per_device // 2
    column_ids = jnp.arange(PANEL, dtype=jnp.int32)
    owners = jnp.take(owner_map, column_ids % devices)
    gathered_ids = (
        (owners % grid_cols) * grid_rows + owners // grid_cols
    ) * (2 * half_slots) + column_ids // devices
    pair_ids = jnp.concatenate([gathered_ids, gathered_ids + half_slots])
    later = jnp.take(owner_map, (column_ids + PANEL) % devices)
    later_ids = (
        (later % grid_cols) * grid_rows + later // grid_cols
    ) * (2 * half_slots) + column_ids // devices
    later_ids = jnp.concatenate([later_ids, later_ids + half_slots])

    def panel_half(h):
        first = first_slot + h * half_slots
        rows = jnp.concatenate(
            [
                lax.dynamic_slice_in_dim(left_vecs, first, half_slots, 0),
                lax.dynamic_slice_in_dim(right_vecs, first, half_slots, 0),
            ],
            axis=0,
        )
        return gather_all(rows)

    def image_half(gathered, ids):
        raw = jnp.einsum("gfn,mn->gfm", matrices, gathered, preferred_element_type=jnp.float32)
        ordered = jnp.take(raw, ids, axis=2)
        feature_rows = ordered.shape[1]
        part = ordered.transpose(1, 0, 2).reshape(feature_rows, 4 * PANEL).astype(jnp.bfloat16)
        part = gather_prow(part)
        return lax.all_gather(part, "pcol", axis=0, tiled=True)

    slots = left_vecs.shape[0]
    height = PANEL // devices
    blocks = slots // (grid_rows * height)

    def slot_order(x):
        x = x.reshape(blocks, grid_rows, height, x.shape[1]).transpose(1, 0, 2, 3)
        return x.reshape(slots, x.shape[3])

    gathered_first = panel_half(0)
    gathered_second = panel_half(1)
    both_vecs = jnp.concatenate([left_vecs, right_vecs], axis=0)
    piece = image_half(gathered_first, pair_ids)
    panel_vecs = jnp.take(
        jnp.concatenate([gathered_first, gathered_second], axis=0),
        jnp.concatenate([pair_ids, pair_ids + gathered_first.shape[0]]),
        axis=0,
    )
    panel_prod = jnp.dot(panel_vecs, piece, preferred_element_type=jnp.float32)
    panel_top = combine(panel_prod[:PANEL], panel_prod[PANEL : 2 * PANEL])
    panel_bottom = combine(panel_prod[2 * PANEL : 3 * PANEL], panel_prod[3 * PANEL :])
    prod = jnp.dot(both_vecs, piece, preferred_element_type=jnp.float32)
    schur_first = slot_order(combine(prod[:slots], prod[slots:]))
    piece = image_half(gathered_second, later_ids)
    prod = jnp.dot(both_vecs, piece, preferred_element_type=jnp.float32)
    schur_second = slot_order(combine(prod[:slots], prod[slots:]))
    inverse = block_inverse_factor(panel_top)
    ahead = jnp.dot(
        panel_bottom,
        inverse.T,
        precision=lax.Precision.HIGHEST,
        preferred_element_type=jnp.float32,
    )
    place = jnp.arange(slots, dtype=jnp.int32)
    slot_of = (place % (blocks * height)) // height * (grid_rows * height) + (
        place // (blocks * height)
    ) * height + place % height
    schur_ids = slot_of * devices + residue
    full_t = lax.dot_general(
        inverse,
        schur_first,
        (((1,), (1,)), ((), ())),
        precision=lax.Precision.HIGHEST,
        preferred_element_type=jnp.float32,
    )
    full_t = jnp.where((schur_ids >= start)[None, :], full_t, jnp.float32(0.0))
    update_t = schur_second.T - jnp.dot(
        ahead, full_t, precision=lax.Precision.HIGHEST, preferred_element_type=jnp.float32
    )
    update_t = jnp.where((schur_ids >= start + PANEL)[None, :], update_t, jnp.float32(0.0))
    return relay_rows(full_t, update_t, owner_map, devices, grid_rows)


def solution(mesh):
    return jax.shard_map(
        body,
        mesh=mesh,
        in_specs=(
            P(("prow", "pcol"), None),
            P(("prow", "pcol"), None),
            P(("prow", "pcol"), None),
            P(("prow", "pcol"), None),
            P(),
            P(),
        ),
        out_specs=(P("pcol", "prow"), P("pcol", "prow")),
        check_vma=False,
    )
```

```python
import jax
import jax.numpy as jnp
from jax import lax
from jax.sharding import PartitionSpec as P


PANEL = 256


def combine(left_prod, right_prod):
    seg = left_prod.shape[1] // 4
    return (
        left_prod[:, seg : 2 * seg] * right_prod[:, 2 * seg : 3 * seg]
        + right_prod[:, seg : 2 * seg] * left_prod[:, 2 * seg : 3 * seg]
        + left_prod[:, 0:seg] * right_prod[:, 3 * seg : 4 * seg]
        + right_prod[:, 0:seg] * left_prod[:, 3 * seg : 4 * seg]
    )


def gather_prow(x, axis=0):
    size = lax.axis_size("prow")
    me = lax.axis_index("prow")
    step = 1
    while step < size:
        got = lax.ppermute(x, "prow", perm=[(i, i ^ step) for i in range(size)])
        low = (me & step) == 0
        x = jnp.where(
            low, jnp.concatenate([x, got], axis=axis), jnp.concatenate([got, x], axis=axis)
        )
        step *= 2
    return x


def gather_all(x):
    return lax.all_gather(gather_prow(x), "pcol", axis=0, tiled=True)


def mm(a, b):
    return jnp.dot(a, b, precision=lax.Precision.HIGHEST, preferred_element_type=jnp.float32)


def block_inverse_factor(base):
    half = base.shape[0] // 2
    eye = jnp.eye(half, dtype=jnp.float32)
    sym = (base + base.T) * jnp.float32(0.5)
    first = jnp.linalg.cholesky(sym[:half, :half], symmetrize_input=False)
    first_inv = lax.linalg.triangular_solve(first, eye, left_side=True, lower=True)
    lower = mm(sym[half:, :half], first_inv.T)
    second = jnp.linalg.cholesky(sym[half:, half:] - mm(lower, lower.T), symmetrize_input=False)
    second_inv = lax.linalg.triangular_solve(second, eye, left_side=True, lower=True)
    corner = -mm(second_inv, mm(lower, first_inv))
    top = jnp.concatenate([first_inv, jnp.zeros_like(first_inv)], axis=1)
    return jnp.concatenate([top, jnp.concatenate([corner, second_inv], axis=1)], axis=0)


def relay_rows(full_t, update_t, owner_map, devices, grid_rows):
    cols, slots = full_t.shape
    grid_cols = devices // grid_rows
    per_row = slots // grid_rows
    both = jnp.stack(
        [full_t.reshape(cols, grid_rows, per_row), update_t.reshape(cols, grid_rows, per_row)],
        axis=2,
    ).reshape(cols, grid_rows, 2 * per_row)
    outgoing = both.transpose(1, 0, 2).reshape(devices, cols // grid_cols * 2 * per_row)
    arrived = lax.all_to_all(outgoing, ("prow", "pcol"), split_axis=0, concat_axis=0, tiled=True)
    ordered = jnp.take(arrived, owner_map, axis=0).T
    narrow = cols // grid_cols
    placed = ordered.reshape(narrow, 2, per_row * devices).transpose(1, 0, 2)
    return (placed[0], placed[1])


def body(left_vecs, right_vecs, primal, dual_inverse, owner_map, panel_index):
    devices = lax.axis_size(("prow", "pcol"))
    grid_rows = lax.axis_size("prow")
    grid_cols = lax.axis_size("pcol")
    per_device = 2 * PANEL // devices
    start = panel_index[0] * PANEL
    first_slot = start // devices
    me = lax.axis_index("prow") * grid_cols + lax.axis_index("pcol")
    residue = jnp.sum(jnp.where(owner_map == me, jnp.arange(devices, dtype=jnp.int32), 0))
    moves = [
        ((q * grid_rows + p), (p * grid_cols + q))
        for p in range(grid_rows)
        for q in range(grid_cols)
    ]
    matrices = lax.ppermute(
        jnp.stack([primal, dual_inverse], axis=0), ("prow", "pcol"), perm=moves
    )
    half_slots = per_device // 2
    column_ids = jnp.arange(PANEL, dtype=jnp.int32)
    owners = jnp.take(owner_map, column_ids % devices)
    gathered_ids = (
        (owners % grid_cols) * grid_rows + owners // grid_cols
    ) * (2 * half_slots) + column_ids // devices
    pair_ids = jnp.concatenate([gathered_ids, gathered_ids + half_slots])
    later = jnp.take(owner_map, (column_ids + PANEL) % devices)
    later_ids = (
        (later % grid_cols) * grid_rows + later // grid_cols
    ) * (2 * half_slots) + column_ids // devices
    later_ids = jnp.concatenate([later_ids, later_ids + half_slots])

    def panel_half(h):
        first = first_slot + h * half_slots
        rows = jnp.concatenate(
            [
                lax.dynamic_slice_in_dim(left_vecs, first, half_slots, 0),
                lax.dynamic_slice_in_dim(right_vecs, first, half_slots, 0),
            ],
            axis=0,
        )
        return gather_all(rows)

    def image_half(gathered, ids):
        raw = jnp.einsum("gfn,mn->gfm", matrices, gathered, preferred_element_type=jnp.float32)
        ordered = jnp.take(raw, ids, axis=2)
        feature_rows = ordered.shape[1]
        part = ordered.transpose(1, 0, 2).reshape(feature_rows, 4 * PANEL).astype(jnp.bfloat16)
        part = gather_prow(part)
        return lax.all_gather(part, "pcol", axis=0, tiled=True)

    slots = left_vecs.shape[0]
    height = PANEL // devices
    blocks = slots // (grid_rows * height)

    def slot_order(x):
        x = x.reshape(blocks, grid_rows, height, x.shape[1]).transpose(1, 0, 2, 3)
        return x.reshape(slots, x.shape[3])

    gathered_first = panel_half(0)
    gathered_second = panel_half(1)
    both_vecs = jnp.concatenate([left_vecs, right_vecs], axis=0)
    piece = image_half(gathered_first, pair_ids)
    panel_prod = jnp.dot(gathered_first, piece, preferred_element_type=jnp.float32)
    panel_top = combine(
        jnp.take(panel_prod, pair_ids[:PANEL], axis=0),
        jnp.take(panel_prod, pair_ids[PANEL:], axis=0),
    )
    panel_prod = jnp.dot(gathered_second, piece, preferred_element_type=jnp.float32)
    panel_bottom = combine(
        jnp.take(panel_prod, later_ids[:PANEL], axis=0),
        jnp.take(panel_prod, later_ids[PANEL:], axis=0),
    )
    prod = jnp.dot(both_vecs, piece, preferred_element_type=jnp.float32)
    schur_first = slot_order(combine(prod[:slots], prod[slots:]))
    piece = image_half(gathered_second, later_ids)
    prod = jnp.dot(both_vecs, piece, preferred_element_type=jnp.float32)
    schur_second = slot_order(combine(prod[:slots], prod[slots:]))
    inverse = block_inverse_factor(panel_top)
    ahead = jnp.dot(
        panel_bottom,
        inverse.T,
        precision=lax.Precision.HIGHEST,
        preferred_element_type=jnp.float32,
    )
    place = jnp.arange(slots, dtype=jnp.int32)
    slot_of = (place % (blocks * height)) // height * (grid_rows * height) + (
        place // (blocks * height)
    ) * height + place % height
    schur_ids = slot_of * devices + residue
    full_t = lax.dot_general(
        inverse,
        schur_first,
        (((1,), (1,)), ((), ())),
        precision=lax.Precision.HIGHEST,
        preferred_element_type=jnp.float32,
    )
    full_t = jnp.where((schur_ids >= start)[None, :], full_t, jnp.float32(0.0))
    update_t = schur_second.T - jnp.dot(
        ahead, full_t, precision=lax.Precision.HIGHEST, preferred_element_type=jnp.float32
    )
    update_t = jnp.where((schur_ids >= start + PANEL)[None, :], update_t, jnp.float32(0.0))
    return relay_rows(full_t, update_t, owner_map, devices, grid_rows)


def solution(mesh):
    return jax.shard_map(
        body,
        mesh=mesh,
        in_specs=(
            P(("prow", "pcol"), None),
            P(("prow", "pcol"), None),
            P(("prow", "pcol"), None),
            P(("prow", "pcol"), None),
            P(),
            P(),
        ),
        out_specs=(P("pcol", "prow"), P("pcol", "prow")),
        check_vma=False,
    )
```

```python
import jax
import jax.numpy as jnp
from jax import lax
from jax.sharding import PartitionSpec as P


PANEL = 256


def combine(left_prod, right_prod):
    seg = left_prod.shape[1] // 4
    return (
        left_prod[:, seg : 2 * seg] * right_prod[:, 2 * seg : 3 * seg]
        + right_prod[:, seg : 2 * seg] * left_prod[:, 2 * seg : 3 * seg]
        + left_prod[:, 0:seg] * right_prod[:, 3 * seg : 4 * seg]
        + right_prod[:, 0:seg] * left_prod[:, 3 * seg : 4 * seg]
    )


def gather_prow(x, axis=0):
    size = lax.axis_size("prow")
    me = lax.axis_index("prow")
    step = 1
    while step < size:
        got = lax.ppermute(x, "prow", perm=[(i, i ^ step) for i in range(size)])
        low = (me & step) == 0
        x = jnp.where(
            low, jnp.concatenate([x, got], axis=axis), jnp.concatenate([got, x], axis=axis)
        )
        step *= 2
    return x


def gather_all(x):
    return lax.all_gather(gather_prow(x), "pcol", axis=0, tiled=True)


def mm(a, b):
    return jnp.dot(a, b, precision=lax.Precision.HIGHEST, preferred_element_type=jnp.float32)


def block_inverse_factor(base):
    half = base.shape[0] // 2
    eye = jnp.eye(half, dtype=jnp.float32)
    sym = (base + base.T) * jnp.float32(0.5)
    first = jnp.linalg.cholesky(sym[:half, :half], symmetrize_input=False)
    first_inv = lax.linalg.triangular_solve(first, eye, left_side=True, lower=True)
    lower = mm(sym[half:, :half], first_inv.T)
    second = jnp.linalg.cholesky(sym[half:, half:] - mm(lower, lower.T), symmetrize_input=False)
    second_inv = lax.linalg.triangular_solve(second, eye, left_side=True, lower=True)
    corner = -mm(second_inv, mm(lower, first_inv))
    top = jnp.concatenate([first_inv, jnp.zeros_like(first_inv)], axis=1)
    return jnp.concatenate([top, jnp.concatenate([corner, second_inv], axis=1)], axis=0)


def relay_rows(part_t, owner_map, devices, grid_rows):
    cols, slots = part_t.shape
    grid_cols = devices // grid_rows
    per_row = slots // grid_rows
    outgoing = part_t.reshape(cols, grid_rows, per_row).transpose(1, 0, 2)
    outgoing = outgoing.reshape(devices, cols // grid_cols * per_row)
    arrived = lax.all_to_all(outgoing, ("prow", "pcol"), split_axis=0, concat_axis=0, tiled=True)
    ordered = jnp.take(arrived, owner_map, axis=0).T
    return ordered.reshape(cols // grid_cols, per_row * devices)


def body(left_vecs, right_vecs, primal, dual_inverse, owner_map, panel_index):
    devices = lax.axis_size(("prow", "pcol"))
    grid_rows = lax.axis_size("prow")
    grid_cols = lax.axis_size("pcol")
    per_device = 2 * PANEL // devices
    start = panel_index[0] * PANEL
    first_slot = start // devices
    me = lax.axis_index("prow") * grid_cols + lax.axis_index("pcol")
    residue = jnp.sum(jnp.where(owner_map == me, jnp.arange(devices, dtype=jnp.int32), 0))
    moves = [
        ((q * grid_rows + p), (p * grid_cols + q))
        for p in range(grid_rows)
        for q in range(grid_cols)
    ]
    matrices = lax.ppermute(
        jnp.stack([primal, dual_inverse], axis=0), ("prow", "pcol"), perm=moves
    )
    half_slots = per_device // 2
    column_ids = jnp.arange(PANEL, dtype=jnp.int32)
    owners = jnp.take(owner_map, column_ids % devices)
    gathered_ids = (
        (owners % grid_cols) * grid_rows + owners // grid_cols
    ) * (2 * half_slots) + column_ids // devices
    pair_ids = jnp.concatenate([gathered_ids, gathered_ids + half_slots])
    later = jnp.take(owner_map, (column_ids + PANEL) % devices)
    later_ids = (
        (later % grid_cols) * grid_rows + later // grid_cols
    ) * (2 * half_slots) + column_ids // devices
    later_ids = jnp.concatenate([later_ids, later_ids + half_slots])

    def panel_half(h):
        first = first_slot + h * half_slots
        rows = jnp.concatenate(
            [
                lax.dynamic_slice_in_dim(left_vecs, first, half_slots, 0),
                lax.dynamic_slice_in_dim(right_vecs, first, half_slots, 0),
            ],
            axis=0,
        )
        return gather_all(rows)

    def image_half(gathered, ids):
        raw = jnp.einsum("gfn,mn->gfm", matrices, gathered, preferred_element_type=jnp.float32)
        ordered = jnp.take(raw, ids, axis=2)
        feature_rows = ordered.shape[1]
        part = ordered.transpose(1, 0, 2).reshape(feature_rows, 4 * PANEL).astype(jnp.bfloat16)
        part = gather_prow(part)
        return lax.all_gather(part, "pcol", axis=0, tiled=True)

    slots = left_vecs.shape[0]
    height = PANEL // devices
    blocks = slots // (grid_rows * height)

    def slot_order(x):
        x = x.reshape(blocks, grid_rows, height, x.shape[1]).transpose(1, 0, 2, 3)
        return x.reshape(slots, x.shape[3])

    gathered_first = panel_half(0)
    gathered_second = panel_half(1)
    both_vecs = jnp.concatenate([left_vecs, right_vecs], axis=0)
    piece = image_half(gathered_first, pair_ids)
    panel_vecs = jnp.take(
        jnp.concatenate([gathered_first, gathered_second], axis=0),
        jnp.concatenate([pair_ids, pair_ids + gathered_first.shape[0]]),
        axis=0,
    )
    panel_prod = jnp.dot(panel_vecs, piece, preferred_element_type=jnp.float32)
    panel_top = combine(panel_prod[:PANEL], panel_prod[PANEL : 2 * PANEL])
    panel_bottom = combine(panel_prod[2 * PANEL : 3 * PANEL], panel_prod[3 * PANEL :])
    prod = jnp.dot(both_vecs, piece, preferred_element_type=jnp.float32)
    schur_first = slot_order(combine(prod[:slots], prod[slots:]))
    piece = image_half(gathered_second, later_ids)
    prod = jnp.dot(both_vecs, piece, preferred_element_type=jnp.float32)
    schur_second = slot_order(combine(prod[:slots], prod[slots:]))
    inverse = block_inverse_factor(panel_top)
    ahead = jnp.dot(
        panel_bottom,
        inverse.T,
        precision=lax.Precision.HIGHEST,
        preferred_element_type=jnp.float32,
    )
    place = jnp.arange(slots, dtype=jnp.int32)
    slot_of = (place % (blocks * height)) // height * (grid_rows * height) + (
        place // (blocks * height)
    ) * height + place % height
    schur_ids = slot_of * devices + residue
    full_t = lax.dot_general(
        inverse,
        schur_first,
        (((1,), (1,)), ((), ())),
        precision=lax.Precision.HIGHEST,
        preferred_element_type=jnp.float32,
    )
    full_t = jnp.where((schur_ids >= start)[None, :], full_t, jnp.float32(0.0))
    update_t = schur_second.T - jnp.dot(
        ahead, full_t, precision=lax.Precision.HIGHEST, preferred_element_type=jnp.float32
    )
    update_t = jnp.where((schur_ids >= start + PANEL)[None, :], update_t, jnp.float32(0.0))
    return (
        relay_rows(full_t, owner_map, devices, grid_rows),
        relay_rows(update_t, owner_map, devices, grid_rows),
    )


def solution(mesh):
    return jax.shard_map(
        body,
        mesh=mesh,
        in_specs=(
            P(("prow", "pcol"), None),
            P(("prow", "pcol"), None),
            P(("prow", "pcol"), None),
            P(("prow", "pcol"), None),
            P(),
            P(),
        ),
        out_specs=(P("pcol", "prow"), P("pcol", "prow")),
        check_vma=False,
    )
```

```python
import jax
import jax.numpy as jnp
from jax import lax
from jax.sharding import PartitionSpec as P


PANEL = 256


def combine(left_prod, right_prod):
    seg = left_prod.shape[1] // 4
    return (
        left_prod[:, seg : 2 * seg] * right_prod[:, 2 * seg : 3 * seg]
        + right_prod[:, seg : 2 * seg] * left_prod[:, 2 * seg : 3 * seg]
        + left_prod[:, 0:seg] * right_prod[:, 3 * seg : 4 * seg]
        + right_prod[:, 0:seg] * left_prod[:, 3 * seg : 4 * seg]
    )


def gather_prow(x, axis=0):
    size = lax.axis_size("prow")
    me = lax.axis_index("prow")
    step = 1
    while step < size:
        got = lax.ppermute(x, "prow", perm=[(i, i ^ step) for i in range(size)])
        low = (me & step) == 0
        x = jnp.where(
            low, jnp.concatenate([x, got], axis=axis), jnp.concatenate([got, x], axis=axis)
        )
        step *= 2
    return x


def gather_all(x):
    return lax.all_gather(gather_prow(x), "pcol", axis=0, tiled=True)


def mm(a, b):
    return jnp.dot(a, b, precision=lax.Precision.HIGHEST, preferred_element_type=jnp.float32)


def inverse_factor(base, leaf):
    size = base.shape[0]
    if size <= leaf:
        eye = jnp.eye(size, dtype=jnp.float32)
        factor = jnp.linalg.cholesky(base, symmetrize_input=False)
        return lax.linalg.triangular_solve(factor, eye, left_side=True, lower=True)
    half = size // 2
    first_inv = inverse_factor(base[:half, :half], leaf)
    lower = mm(base[half:, :half], first_inv.T)
    second_inv = inverse_factor(base[half:, half:] - mm(lower, lower.T), leaf)
    corner = -mm(second_inv, mm(lower, first_inv))
    top = jnp.concatenate([first_inv, jnp.zeros_like(first_inv)], axis=1)
    return jnp.concatenate([top, jnp.concatenate([corner, second_inv], axis=1)], axis=0)


def block_inverse_factor(base):
    return inverse_factor((base + base.T) * jnp.float32(0.5), base.shape[0] // 4)


def relay_rows(full_t, update_t, owner_map, devices, grid_rows):
    cols, slots = full_t.shape
    grid_cols = devices // grid_rows
    per_row = slots // grid_rows
    both = jnp.stack(
        [full_t.reshape(cols, grid_rows, per_row), update_t.reshape(cols, grid_rows, per_row)],
        axis=2,
    ).reshape(cols, grid_rows, 2 * per_row)
    outgoing = both.transpose(1, 0, 2).reshape(devices, cols // grid_cols * 2 * per_row)
    arrived = lax.all_to_all(outgoing, ("prow", "pcol"), split_axis=0, concat_axis=0, tiled=True)
    ordered = jnp.take(arrived, owner_map, axis=0).T
    narrow = cols // grid_cols
    placed = ordered.reshape(narrow, 2, per_row * devices).transpose(1, 0, 2)
    return (placed[0], placed[1])


def body(left_vecs, right_vecs, primal, dual_inverse, owner_map, panel_index):
    devices = lax.axis_size(("prow", "pcol"))
    grid_rows = lax.axis_size("prow")
    grid_cols = lax.axis_size("pcol")
    per_device = 2 * PANEL // devices
    start = panel_index[0] * PANEL
    first_slot = start // devices
    me = lax.axis_index("prow") * grid_cols + lax.axis_index("pcol")
    residue = jnp.sum(jnp.where(owner_map == me, jnp.arange(devices, dtype=jnp.int32), 0))
    moves = [
        ((q * grid_rows + p), (p * grid_cols + q))
        for p in range(grid_rows)
        for q in range(grid_cols)
    ]
    matrices = lax.ppermute(
        jnp.stack([primal, dual_inverse], axis=0), ("prow", "pcol"), perm=moves
    )
    half_slots = per_device // 2
    column_ids = jnp.arange(PANEL, dtype=jnp.int32)
    owners = jnp.take(owner_map, column_ids % devices)
    gathered_ids = (
        (owners % grid_cols) * grid_rows + owners // grid_cols
    ) * (2 * half_slots) + column_ids // devices
    pair_ids = jnp.concatenate([gathered_ids, gathered_ids + half_slots])
    later = jnp.take(owner_map, (column_ids + PANEL) % devices)
    later_ids = (
        (later % grid_cols) * grid_rows + later // grid_cols
    ) * (2 * half_slots) + column_ids // devices
    later_ids = jnp.concatenate([later_ids, later_ids + half_slots])

    def panel_half(h):
        first = first_slot + h * half_slots
        rows = jnp.concatenate(
            [
                lax.dynamic_slice_in_dim(left_vecs, first, half_slots, 0),
                lax.dynamic_slice_in_dim(right_vecs, first, half_slots, 0),
            ],
            axis=0,
        )
        return gather_all(rows)

    def image_half(gathered, ids):
        raw = jnp.einsum("gfn,mn->gfm", matrices, gathered, preferred_element_type=jnp.float32)
        ordered = jnp.take(raw, ids, axis=2)
        feature_rows = ordered.shape[1]
        part = ordered.transpose(1, 0, 2).reshape(feature_rows, 4 * PANEL).astype(jnp.bfloat16)
        part = gather_prow(part)
        return lax.all_gather(part, "pcol", axis=0, tiled=True)

    slots = left_vecs.shape[0]
    height = PANEL // devices
    blocks = slots // (grid_rows * height)

    def slot_order(x):
        x = x.reshape(blocks, grid_rows, height, x.shape[1]).transpose(1, 0, 2, 3)
        return x.reshape(slots, x.shape[3])

    gathered_first = panel_half(0)
    gathered_second = panel_half(1)
    both_vecs = jnp.concatenate([left_vecs, right_vecs], axis=0)
    piece = image_half(gathered_first, pair_ids)
    panel_vecs = jnp.take(
        jnp.concatenate([gathered_first, gathered_second], axis=0),
        jnp.concatenate([pair_ids, pair_ids + gathered_first.shape[0]]),
        axis=0,
    )
    panel_prod = jnp.dot(panel_vecs, piece, preferred_element_type=jnp.float32)
    panel_top = combine(panel_prod[:PANEL], panel_prod[PANEL : 2 * PANEL])
    panel_bottom = combine(panel_prod[2 * PANEL : 3 * PANEL], panel_prod[3 * PANEL :])
    prod = jnp.dot(both_vecs, piece, preferred_element_type=jnp.float32)
    schur_first = slot_order(combine(prod[:slots], prod[slots:]))
    piece = image_half(gathered_second, later_ids)
    prod = jnp.dot(both_vecs, piece, preferred_element_type=jnp.float32)
    schur_second = slot_order(combine(prod[:slots], prod[slots:]))
    inverse = block_inverse_factor(panel_top)
    ahead = jnp.dot(
        panel_bottom,
        inverse.T,
        precision=lax.Precision.HIGHEST,
        preferred_element_type=jnp.float32,
    )
    place = jnp.arange(slots, dtype=jnp.int32)
    slot_of = (place % (blocks * height)) // height * (grid_rows * height) + (
        place // (blocks * height)
    ) * height + place % height
    schur_ids = slot_of * devices + residue
    full_t = lax.dot_general(
        inverse,
        schur_first,
        (((1,), (1,)), ((), ())),
        precision=lax.Precision.HIGHEST,
        preferred_element_type=jnp.float32,
    )
    full_t = jnp.where((schur_ids >= start)[None, :], full_t, jnp.float32(0.0))
    update_t = schur_second.T - jnp.dot(
        ahead, full_t, precision=lax.Precision.HIGHEST, preferred_element_type=jnp.float32
    )
    update_t = jnp.where((schur_ids >= start + PANEL)[None, :], update_t, jnp.float32(0.0))
    return relay_rows(full_t, update_t, owner_map, devices, grid_rows)


def solution(mesh):
    return jax.shard_map(
        body,
        mesh=mesh,
        in_specs=(
            P(("prow", "pcol"), None),
            P(("prow", "pcol"), None),
            P(("prow", "pcol"), None),
            P(("prow", "pcol"), None),
            P(),
            P(),
        ),
        out_specs=(P("pcol", "prow"), P("pcol", "prow")),
        check_vma=False,
    )
```

```python
import jax
import jax.numpy as jnp
from jax import lax
from jax.sharding import PartitionSpec as P


PANEL = 256


def combine(left_prod, right_prod):
    seg = left_prod.shape[1] // 4
    return (
        left_prod[:, seg : 2 * seg] * right_prod[:, 2 * seg : 3 * seg]
        + right_prod[:, seg : 2 * seg] * left_prod[:, 2 * seg : 3 * seg]
        + left_prod[:, 0:seg] * right_prod[:, 3 * seg : 4 * seg]
        + right_prod[:, 0:seg] * left_prod[:, 3 * seg : 4 * seg]
    )


def gather_prow(x, axis=0):
    size = lax.axis_size("prow")
    me = lax.axis_index("prow")
    step = 1
    while step < size:
        got = lax.ppermute(x, "prow", perm=[(i, i ^ step) for i in range(size)])
        low = (me & step) == 0
        x = jnp.where(
            low, jnp.concatenate([x, got], axis=axis), jnp.concatenate([got, x], axis=axis)
        )
        step *= 2
    return x


def mm(a, b):
    return jnp.dot(a, b, precision=lax.Precision.HIGHEST, preferred_element_type=jnp.float32)


def block_inverse_factor(base):
    half = base.shape[0] // 2
    eye = jnp.eye(half, dtype=jnp.float32)
    sym = (base + base.T) * jnp.float32(0.5)
    first = jnp.linalg.cholesky(sym[:half, :half], symmetrize_input=False)
    first_inv = lax.linalg.triangular_solve(first, eye, left_side=True, lower=True)
    lower = mm(sym[half:, :half], first_inv.T)
    second = jnp.linalg.cholesky(sym[half:, half:] - mm(lower, lower.T), symmetrize_input=False)
    second_inv = lax.linalg.triangular_solve(second, eye, left_side=True, lower=True)
    corner = -mm(second_inv, mm(lower, first_inv))
    top = jnp.concatenate([first_inv, jnp.zeros_like(first_inv)], axis=1)
    return jnp.concatenate([top, jnp.concatenate([corner, second_inv], axis=1)], axis=0)


def relay_rows(full_t, update_t, owner_map, devices, grid_rows):
    cols, slots = full_t.shape
    grid_cols = devices // grid_rows
    per_row = slots // grid_rows
    both = jnp.stack(
        [full_t.reshape(cols, grid_rows, per_row), update_t.reshape(cols, grid_rows, per_row)],
        axis=2,
    ).reshape(cols, grid_rows, 2 * per_row)
    outgoing = both.transpose(1, 0, 2).reshape(devices, cols // grid_cols * 2 * per_row)
    arrived = lax.all_to_all(outgoing, ("prow", "pcol"), split_axis=0, concat_axis=0, tiled=True)
    ordered = jnp.take(arrived, owner_map, axis=0).T
    narrow = cols // grid_cols
    placed = ordered.reshape(narrow, 2, per_row * devices).transpose(1, 0, 2)
    return (placed[0], placed[1])


def body(left_vecs, right_vecs, primal, dual_inverse, owner_map, panel_index):
    devices = lax.axis_size(("prow", "pcol"))
    grid_rows = lax.axis_size("prow")
    grid_cols = lax.axis_size("pcol")
    per_device = 2 * PANEL // devices
    start = panel_index[0] * PANEL
    first_slot = start // devices
    me = lax.axis_index("prow") * grid_cols + lax.axis_index("pcol")
    residue = jnp.sum(jnp.where(owner_map == me, jnp.arange(devices, dtype=jnp.int32), 0))
    moves = [
        ((q * grid_rows + p), (p * grid_cols + q))
        for p in range(grid_rows)
        for q in range(grid_cols)
    ]
    matrices = lax.ppermute(
        jnp.stack([primal, dual_inverse], axis=0), ("prow", "pcol"), perm=moves
    )
    half_slots = per_device // 2
    column_ids = jnp.arange(PANEL, dtype=jnp.int32)
    owners = jnp.take(owner_map, column_ids % devices)
    gathered_ids = (
        (owners % grid_cols) * grid_rows + owners // grid_cols
    ) * (2 * half_slots) + column_ids // devices
    pair_ids = jnp.concatenate([gathered_ids, gathered_ids + half_slots])
    later = jnp.take(owner_map, (column_ids + PANEL) % devices)
    later_ids = (
        (later % grid_cols) * grid_rows + later // grid_cols
    ) * (2 * half_slots) + column_ids // devices
    later_ids = jnp.concatenate([later_ids, later_ids + half_slots])

    panel_rows = gather_prow(
        jnp.concatenate(
            [
                lax.dynamic_slice_in_dim(left_vecs, first_slot, per_device, 0),
                lax.dynamic_slice_in_dim(right_vecs, first_slot, per_device, 0),
            ],
            axis=0,
        )
    )
    panel_rows = panel_rows.reshape(grid_rows, 2, 2, half_slots, panel_rows.shape[1])

    def panel_half(h):
        rows = panel_rows[:, :, h].reshape(grid_rows * 2 * half_slots, panel_rows.shape[4])
        return lax.all_gather(rows, "pcol", axis=0, tiled=True)

    def image_half(gathered, ids):
        raw = jnp.einsum("gfn,mn->gfm", matrices, gathered, preferred_element_type=jnp.float32)
        ordered = jnp.take(raw, ids, axis=2)
        feature_rows = ordered.shape[1]
        part = ordered.transpose(1, 0, 2).reshape(feature_rows, 4 * PANEL).astype(jnp.bfloat16)
        part = gather_prow(part)
        return lax.all_gather(part, "pcol", axis=0, tiled=True)

    slots = left_vecs.shape[0]
    height = PANEL // devices
    blocks = slots // (grid_rows * height)

    def slot_order(x):
        x = x.reshape(blocks, grid_rows, height, x.shape[1]).transpose(1, 0, 2, 3)
        return x.reshape(slots, x.shape[3])

    gathered_first = panel_half(0)
    gathered_second = panel_half(1)
    both_vecs = jnp.concatenate([left_vecs, right_vecs], axis=0)
    piece = image_half(gathered_first, pair_ids)
    panel_vecs = jnp.take(
        jnp.concatenate([gathered_first, gathered_second], axis=0),
        jnp.concatenate([pair_ids, pair_ids + gathered_first.shape[0]]),
        axis=0,
    )
    panel_prod = jnp.dot(panel_vecs, piece, preferred_element_type=jnp.float32)
    panel_top = combine(panel_prod[:PANEL], panel_prod[PANEL : 2 * PANEL])
    panel_bottom = combine(panel_prod[2 * PANEL : 3 * PANEL], panel_prod[3 * PANEL :])
    prod = jnp.dot(both_vecs, piece, preferred_element_type=jnp.float32)
    schur_first = slot_order(combine(prod[:slots], prod[slots:]))
    piece = image_half(gathered_second, later_ids)
    prod = jnp.dot(both_vecs, piece, preferred_element_type=jnp.float32)
    schur_second = slot_order(combine(prod[:slots], prod[slots:]))
    inverse = block_inverse_factor(panel_top)
    ahead = jnp.dot(
        panel_bottom,
        inverse.T,
        precision=lax.Precision.HIGHEST,
        preferred_element_type=jnp.float32,
    )
    place = jnp.arange(slots, dtype=jnp.int32)
    slot_of = (place % (blocks * height)) // height * (grid_rows * height) + (
        place // (blocks * height)
    ) * height + place % height
    schur_ids = slot_of * devices + residue
    full_t = lax.dot_general(
        inverse,
        schur_first,
        (((1,), (1,)), ((), ())),
        precision=lax.Precision.HIGHEST,
        preferred_element_type=jnp.float32,
    )
    full_t = jnp.where((schur_ids >= start)[None, :], full_t, jnp.float32(0.0))
    update_t = schur_second.T - jnp.dot(
        ahead, full_t, precision=lax.Precision.HIGHEST, preferred_element_type=jnp.float32
    )
    update_t = jnp.where((schur_ids >= start + PANEL)[None, :], update_t, jnp.float32(0.0))
    return relay_rows(full_t, update_t, owner_map, devices, grid_rows)


def solution(mesh):
    return jax.shard_map(
        body,
        mesh=mesh,
        in_specs=(
            P(("prow", "pcol"), None),
            P(("prow", "pcol"), None),
            P(("prow", "pcol"), None),
            P(("prow", "pcol"), None),
            P(),
            P(),
        ),
        out_specs=(P("pcol", "prow"), P("pcol", "prow")),
        check_vma=False,
    )
```

```python
import jax
import jax.numpy as jnp
from jax import lax
from jax.sharding import PartitionSpec as P


PANEL = 256


def combine(left_prod, right_prod):
    seg = left_prod.shape[1] // 4
    return (
        left_prod[:, seg : 2 * seg] * right_prod[:, 2 * seg : 3 * seg]
        + right_prod[:, seg : 2 * seg] * left_prod[:, 2 * seg : 3 * seg]
        + left_prod[:, 0:seg] * right_prod[:, 3 * seg : 4 * seg]
        + right_prod[:, 0:seg] * left_prod[:, 3 * seg : 4 * seg]
    )


def gather_prow(x, axis=0):
    size = lax.axis_size("prow")
    me = lax.axis_index("prow")
    step = 1
    while step < size:
        got = lax.ppermute(x, "prow", perm=[(i, i ^ step) for i in range(size)])
        low = (me & step) == 0
        x = jnp.where(
            low, jnp.concatenate([x, got], axis=axis), jnp.concatenate([got, x], axis=axis)
        )
        step *= 2
    return x


def gather_all(x):
    return lax.all_gather(gather_prow(x), "pcol", axis=0, tiled=True)


def mm(a, b):
    return jnp.dot(a, b, precision=lax.Precision.HIGHEST, preferred_element_type=jnp.float32)


def block_inverse_factor(base):
    half = base.shape[0] // 2
    eye = jnp.eye(half, dtype=jnp.float32)
    sym = (base + base.T) * jnp.float32(0.5)
    first = jnp.linalg.cholesky(sym[:half, :half], symmetrize_input=False)
    first_inv = lax.linalg.triangular_solve(first, eye, left_side=True, lower=True)
    lower = mm(sym[half:, :half], first_inv.T)
    second = jnp.linalg.cholesky(sym[half:, half:] - mm(lower, lower.T), symmetrize_input=False)
    second_inv = lax.linalg.triangular_solve(second, eye, left_side=True, lower=True)
    corner = -mm(second_inv, mm(lower, first_inv))
    top = jnp.concatenate([first_inv, jnp.zeros_like(first_inv)], axis=1)
    return jnp.concatenate([top, jnp.concatenate([corner, second_inv], axis=1)], axis=0)


def relay_rows(full_t, update_t, owner_map, devices, grid_rows):
    cols, slots = full_t.shape
    grid_cols = devices // grid_rows
    per_row = slots // grid_rows
    both = jnp.stack(
        [full_t.reshape(cols, grid_rows, per_row), update_t.reshape(cols, grid_rows, per_row)],
        axis=2,
    ).reshape(cols, grid_rows, 2 * per_row)
    outgoing = both.transpose(1, 0, 2).reshape(devices, cols // grid_cols * 2 * per_row)
    arrived = lax.all_to_all(outgoing, ("prow", "pcol"), split_axis=0, concat_axis=0, tiled=True)
    narrow = cols // grid_cols
    ordered = jnp.take(arrived, owner_map, axis=0).reshape(devices, narrow, 2, per_row)
    return tuple(
        ordered[:, :, w, :].transpose(1, 2, 0).reshape(narrow, per_row * devices) for w in range(2)
    )


def body(left_vecs, right_vecs, primal, dual_inverse, owner_map, panel_index):
    devices = lax.axis_size(("prow", "pcol"))
    grid_rows = lax.axis_size("prow")
    grid_cols = lax.axis_size("pcol")
    per_device = 2 * PANEL // devices
    start = panel_index[0] * PANEL
    first_slot = start // devices
    me = lax.axis_index("prow") * grid_cols + lax.axis_index("pcol")
    residue = jnp.sum(jnp.where(owner_map == me, jnp.arange(devices, dtype=jnp.int32), 0))
    moves = [
        ((q * grid_rows + p), (p * grid_cols + q))
        for p in range(grid_rows)
        for q in range(grid_cols)
    ]
    matrices = lax.ppermute(
        jnp.stack([primal, dual_inverse], axis=0), ("prow", "pcol"), perm=moves
    )
    half_slots = per_device // 2
    column_ids = jnp.arange(PANEL, dtype=jnp.int32)
    owners = jnp.take(owner_map, column_ids % devices)
    gathered_ids = (
        (owners % grid_cols) * grid_rows + owners // grid_cols
    ) * (2 * half_slots) + column_ids // devices
    pair_ids = jnp.concatenate([gathered_ids, gathered_ids + half_slots])
    later = jnp.take(owner_map, (column_ids + PANEL) % devices)
    later_ids = (
        (later % grid_cols) * grid_rows + later // grid_cols
    ) * (2 * half_slots) + column_ids // devices
    later_ids = jnp.concatenate([later_ids, later_ids + half_slots])

    def panel_half(h):
        first = first_slot + h * half_slots
        rows = jnp.concatenate(
            [
                lax.dynamic_slice_in_dim(left_vecs, first, half_slots, 0),
                lax.dynamic_slice_in_dim(right_vecs, first, half_slots, 0),
            ],
            axis=0,
        )
        return gather_all(rows)

    def image_half(gathered, ids):
        raw = jnp.einsum("gfn,mn->gfm", matrices, gathered, preferred_element_type=jnp.float32)
        ordered = jnp.take(raw, ids, axis=2)
        feature_rows = ordered.shape[1]
        part = ordered.transpose(1, 0, 2).reshape(feature_rows, 4 * PANEL).astype(jnp.bfloat16)
        part = gather_prow(part)
        return lax.all_gather(part, "pcol", axis=0, tiled=True)

    slots = left_vecs.shape[0]
    height = PANEL // devices
    blocks = slots // (grid_rows * height)

    def slot_order(x):
        x = x.reshape(blocks, grid_rows, height, x.shape[1]).transpose(1, 0, 2, 3)
        return x.reshape(slots, x.shape[3])

    gathered_first = panel_half(0)
    gathered_second = panel_half(1)
    both_vecs = jnp.concatenate([left_vecs, right_vecs], axis=0)
    piece = image_half(gathered_first, pair_ids)
    panel_vecs = jnp.take(
        jnp.concatenate([gathered_first, gathered_second], axis=0),
        jnp.concatenate([pair_ids, pair_ids + gathered_first.shape[0]]),
        axis=0,
    )
    panel_prod = jnp.dot(panel_vecs, piece, preferred_element_type=jnp.float32)
    panel_top = combine(panel_prod[:PANEL], panel_prod[PANEL : 2 * PANEL])
    panel_bottom = combine(panel_prod[2 * PANEL : 3 * PANEL], panel_prod[3 * PANEL :])
    prod = jnp.dot(both_vecs, piece, preferred_element_type=jnp.float32)
    schur_first = slot_order(combine(prod[:slots], prod[slots:]))
    piece = image_half(gathered_second, later_ids)
    prod = jnp.dot(both_vecs, piece, preferred_element_type=jnp.float32)
    schur_second = slot_order(combine(prod[:slots], prod[slots:]))
    inverse = block_inverse_factor(panel_top)
    ahead = jnp.dot(
        panel_bottom,
        inverse.T,
        precision=lax.Precision.HIGHEST,
        preferred_element_type=jnp.float32,
    )
    place = jnp.arange(slots, dtype=jnp.int32)
    slot_of = (place % (blocks * height)) // height * (grid_rows * height) + (
        place // (blocks * height)
    ) * height + place % height
    schur_ids = slot_of * devices + residue
    full_t = lax.dot_general(
        inverse,
        schur_first,
        (((1,), (1,)), ((), ())),
        precision=lax.Precision.HIGHEST,
        preferred_element_type=jnp.float32,
    )
    full_t = jnp.where((schur_ids >= start)[None, :], full_t, jnp.float32(0.0))
    update_t = schur_second.T - jnp.dot(
        ahead, full_t, precision=lax.Precision.HIGHEST, preferred_element_type=jnp.float32
    )
    update_t = jnp.where((schur_ids >= start + PANEL)[None, :], update_t, jnp.float32(0.0))
    return relay_rows(full_t, update_t, owner_map, devices, grid_rows)


def solution(mesh):
    return jax.shard_map(
        body,
        mesh=mesh,
        in_specs=(
            P(("prow", "pcol"), None),
            P(("prow", "pcol"), None),
            P(("prow", "pcol"), None),
            P(("prow", "pcol"), None),
            P(),
            P(),
        ),
        out_specs=(P("pcol", "prow"), P("pcol", "prow")),
        check_vma=False,
    )
```

```python
import jax
import jax.numpy as jnp
from jax import lax
from jax.sharding import PartitionSpec as P


PANEL = 256


def combine(left_prod, right_prod):
    seg = left_prod.shape[1] // 4
    return (
        left_prod[:, seg : 2 * seg] * right_prod[:, 2 * seg : 3 * seg]
        + right_prod[:, seg : 2 * seg] * left_prod[:, 2 * seg : 3 * seg]
        + left_prod[:, 0:seg] * right_prod[:, 3 * seg : 4 * seg]
        + right_prod[:, 0:seg] * left_prod[:, 3 * seg : 4 * seg]
    )


def gather_prow(x, axis=0):
    size = lax.axis_size("prow")
    me = lax.axis_index("prow")
    step = 1
    while step < size:
        got = lax.ppermute(x, "prow", perm=[(i, i ^ step) for i in range(size)])
        low = (me & step) == 0
        x = jnp.where(
            low, jnp.concatenate([x, got], axis=axis), jnp.concatenate([got, x], axis=axis)
        )
        step *= 2
    return x


def gather_all(x):
    return lax.all_gather(gather_prow(x), "pcol", axis=0, tiled=True)


def mm(a, b):
    return jnp.dot(a, b, precision=lax.Precision.HIGHEST, preferred_element_type=jnp.float32)


def block_inverse_factor(base):
    half = base.shape[0] // 2
    eye = jnp.eye(half, dtype=jnp.float32)
    sym = (base + base.T) * jnp.float32(0.5)
    first = jnp.linalg.cholesky(sym[:half, :half], symmetrize_input=False)
    first_inv = lax.linalg.triangular_solve(first, eye, left_side=True, lower=True)
    lower = mm(sym[half:, :half], first_inv.T)
    second = jnp.linalg.cholesky(sym[half:, half:] - mm(lower, lower.T), symmetrize_input=False)
    second_inv = lax.linalg.triangular_solve(second, eye, left_side=True, lower=True)
    corner = -mm(second_inv, mm(lower, first_inv))
    top = jnp.concatenate([first_inv, jnp.zeros_like(first_inv)], axis=1)
    return jnp.concatenate([top, jnp.concatenate([corner, second_inv], axis=1)], axis=0)


def relay_rows(full_t, update_t, owner_map, devices, grid_rows):
    cols, slots = full_t.shape
    grid_cols = devices // grid_rows
    per_row = slots // grid_rows
    both = jnp.stack(
        [full_t.reshape(cols, grid_rows, per_row), update_t.reshape(cols, grid_rows, per_row)],
        axis=2,
    ).reshape(cols, grid_rows, 2 * per_row)
    outgoing = both.transpose(1, 0, 2).reshape(devices, cols // grid_cols * 2 * per_row)
    arrived = lax.all_to_all(outgoing, ("prow", "pcol"), split_axis=0, concat_axis=0, tiled=True)
    narrow = cols // grid_cols
    ordered = jnp.take(arrived, owner_map, axis=0).reshape(devices, narrow, 2, per_row)
    return tuple(
        ordered[:, :, w, :].transpose(1, 2, 0).reshape(narrow, per_row * devices) for w in range(2)
    )


def body(left_vecs, right_vecs, primal, dual_inverse, owner_map, panel_index):
    devices = lax.axis_size(("prow", "pcol"))
    grid_rows = lax.axis_size("prow")
    grid_cols = lax.axis_size("pcol")
    per_device = 2 * PANEL // devices
    start = panel_index[0] * PANEL
    first_slot = start // devices
    me = lax.axis_index("prow") * grid_cols + lax.axis_index("pcol")
    residue = jnp.sum(jnp.where(owner_map == me, jnp.arange(devices, dtype=jnp.int32), 0))
    moves = [
        ((q * grid_rows + p), (p * grid_cols + q))
        for p in range(grid_rows)
        for q in range(grid_cols)
    ]
    matrices = lax.ppermute(
        jnp.stack([primal, dual_inverse], axis=0), ("prow", "pcol"), perm=moves
    )
    half_slots = per_device // 2
    column_ids = jnp.arange(PANEL, dtype=jnp.int32)
    owners = jnp.take(owner_map, column_ids % devices)
    gathered_ids = (
        (owners % grid_cols) * grid_rows + owners // grid_cols
    ) * (2 * half_slots) + column_ids // devices
    pair_ids = jnp.concatenate([gathered_ids, gathered_ids + half_slots])
    later = jnp.take(owner_map, (column_ids + PANEL) % devices)
    later_ids = (
        (later % grid_cols) * grid_rows + later // grid_cols
    ) * (2 * half_slots) + column_ids // devices
    later_ids = jnp.concatenate([later_ids, later_ids + half_slots])

    def panel_half(h):
        first = first_slot + h * half_slots
        rows = jnp.concatenate(
            [
                lax.dynamic_slice_in_dim(left_vecs, first, half_slots, 0),
                lax.dynamic_slice_in_dim(right_vecs, first, half_slots, 0),
            ],
            axis=0,
        )
        return gather_all(rows)

    def image_half(gathered, ids):
        raw = jnp.einsum("gfn,mn->gfm", matrices, gathered, preferred_element_type=jnp.float32)
        ordered = jnp.take(raw, ids, axis=2)
        feature_rows = ordered.shape[1]
        part = ordered.transpose(1, 0, 2).reshape(feature_rows, 4 * PANEL).astype(jnp.bfloat16)
        part = gather_prow(part)
        return lax.all_gather(part, "pcol", axis=0, tiled=True)

    slots = left_vecs.shape[0]
    height = PANEL // devices
    blocks = slots // (grid_rows * height)

    def slot_order(x):
        x = x.reshape(blocks, grid_rows, height, x.shape[1]).transpose(1, 0, 2, 3)
        return x.reshape(slots, x.shape[3])

    gathered_first = panel_half(0)
    gathered_second = panel_half(1)
    both_vecs = jnp.concatenate([left_vecs, right_vecs], axis=0)
    piece = image_half(gathered_first, pair_ids)
    panel_vecs = jnp.take(
        jnp.concatenate([gathered_first, gathered_second], axis=0),
        jnp.concatenate([pair_ids, pair_ids + gathered_first.shape[0]]),
        axis=0,
    )
    panel_prod = jnp.dot(panel_vecs, piece, preferred_element_type=jnp.float32)
    panel_top = combine(panel_prod[:PANEL], panel_prod[PANEL : 2 * PANEL])
    panel_bottom = combine(panel_prod[2 * PANEL : 3 * PANEL], panel_prod[3 * PANEL :])
    prod = jnp.dot(both_vecs, piece, preferred_element_type=jnp.float32)
    schur_first = slot_order(combine(prod[:slots], prod[slots:]))
    piece = image_half(gathered_second, later_ids)
    prod = jnp.dot(both_vecs, piece, preferred_element_type=jnp.float32)
    schur_second = slot_order(combine(prod[:slots], prod[slots:]))
    inverse = block_inverse_factor(panel_top)
    ahead = jnp.dot(
        panel_bottom,
        inverse.T,
        precision=lax.Precision.HIGH,
        preferred_element_type=jnp.float32,
    )
    place = jnp.arange(slots, dtype=jnp.int32)
    slot_of = (place % (blocks * height)) // height * (grid_rows * height) + (
        place // (blocks * height)
    ) * height + place % height
    schur_ids = slot_of * devices + residue
    full_t = lax.dot_general(
        inverse,
        schur_first,
        (((1,), (1,)), ((), ())),
        precision=lax.Precision.HIGH,
        preferred_element_type=jnp.float32,
    )
    full_t = jnp.where((schur_ids >= start)[None, :], full_t, jnp.float32(0.0))
    update_t = schur_second.T - jnp.dot(
        ahead, full_t, precision=lax.Precision.HIGH, preferred_element_type=jnp.float32
    )
    update_t = jnp.where((schur_ids >= start + PANEL)[None, :], update_t, jnp.float32(0.0))
    return relay_rows(full_t, update_t, owner_map, devices, grid_rows)


def solution(mesh):
    return jax.shard_map(
        body,
        mesh=mesh,
        in_specs=(
            P(("prow", "pcol"), None),
            P(("prow", "pcol"), None),
            P(("prow", "pcol"), None),
            P(("prow", "pcol"), None),
            P(),
            P(),
        ),
        out_specs=(P("pcol", "prow"), P("pcol", "prow")),
        check_vma=False,
    )
```

```python
import jax
import jax.numpy as jnp
from jax import lax
from jax.sharding import PartitionSpec as P


PANEL = 256


def combine(left_prod, right_prod):
    seg = left_prod.shape[1] // 4
    return (
        left_prod[:, seg : 2 * seg] * right_prod[:, 2 * seg : 3 * seg]
        + right_prod[:, seg : 2 * seg] * left_prod[:, 2 * seg : 3 * seg]
        + left_prod[:, 0:seg] * right_prod[:, 3 * seg : 4 * seg]
        + right_prod[:, 0:seg] * left_prod[:, 3 * seg : 4 * seg]
    )


def gather_prow(x, axis=0):
    size = lax.axis_size("prow")
    me = lax.axis_index("prow")
    step = 1
    while step < size:
        got = lax.ppermute(x, "prow", perm=[(i, i ^ step) for i in range(size)])
        low = (me & step) == 0
        x = jnp.where(
            low, jnp.concatenate([x, got], axis=axis), jnp.concatenate([got, x], axis=axis)
        )
        step *= 2
    return x


def gather_all(x):
    return lax.all_gather(gather_prow(x), "pcol", axis=0, tiled=True)


def mm(a, b):
    return jnp.dot(a, b, precision=lax.Precision.HIGHEST, preferred_element_type=jnp.float32)


def block_inverse_factor(base):
    half = base.shape[0] // 2
    eye = jnp.eye(half, dtype=jnp.float32)
    sym = (base + base.T) * jnp.float32(0.5)
    first = jnp.linalg.cholesky(sym[:half, :half], symmetrize_input=False)
    first_inv = lax.linalg.triangular_solve(first, eye, left_side=True, lower=True)
    lower = mm(sym[half:, :half], first_inv.T)
    second = jnp.linalg.cholesky(sym[half:, half:] - mm(lower, lower.T), symmetrize_input=False)
    second_inv = lax.linalg.triangular_solve(second, eye, left_side=True, lower=True)
    corner = -jnp.dot(
        second_inv,
        jnp.dot(lower, first_inv, precision=lax.Precision.HIGH, preferred_element_type=jnp.float32),
        precision=lax.Precision.HIGH,
        preferred_element_type=jnp.float32,
    )
    top = jnp.concatenate([first_inv, jnp.zeros_like(first_inv)], axis=1)
    return jnp.concatenate([top, jnp.concatenate([corner, second_inv], axis=1)], axis=0)


def relay_rows(full_t, update_t, owner_map, devices, grid_rows):
    cols, slots = full_t.shape
    grid_cols = devices // grid_rows
    per_row = slots // grid_rows
    both = jnp.stack(
        [full_t.reshape(cols, grid_rows, per_row), update_t.reshape(cols, grid_rows, per_row)],
        axis=2,
    ).reshape(cols, grid_rows, 2 * per_row)
    outgoing = both.transpose(1, 0, 2).reshape(devices, cols // grid_cols * 2 * per_row)
    arrived = lax.all_to_all(outgoing, ("prow", "pcol"), split_axis=0, concat_axis=0, tiled=True)
    narrow = cols // grid_cols
    ordered = jnp.take(arrived, owner_map, axis=0).reshape(devices, narrow, 2, per_row)
    return tuple(
        ordered[:, :, w, :].transpose(1, 2, 0).reshape(narrow, per_row * devices) for w in range(2)
    )


def body(left_vecs, right_vecs, primal, dual_inverse, owner_map, panel_index):
    devices = lax.axis_size(("prow", "pcol"))
    grid_rows = lax.axis_size("prow")
    grid_cols = lax.axis_size("pcol")
    per_device = 2 * PANEL // devices
    start = panel_index[0] * PANEL
    first_slot = start // devices
    me = lax.axis_index("prow") * grid_cols + lax.axis_index("pcol")
    residue = jnp.sum(jnp.where(owner_map == me, jnp.arange(devices, dtype=jnp.int32), 0))
    moves = [
        ((q * grid_rows + p), (p * grid_cols + q))
        for p in range(grid_rows)
        for q in range(grid_cols)
    ]
    matrices = lax.ppermute(
        jnp.stack([primal, dual_inverse], axis=0), ("prow", "pcol"), perm=moves
    )
    half_slots = per_device // 2
    column_ids = jnp.arange(PANEL, dtype=jnp.int32)
    owners = jnp.take(owner_map, column_ids % devices)
    gathered_ids = (
        (owners % grid_cols) * grid_rows + owners // grid_cols
    ) * (2 * half_slots) + column_ids // devices
    pair_ids = jnp.concatenate([gathered_ids, gathered_ids + half_slots])
    later = jnp.take(owner_map, (column_ids + PANEL) % devices)
    later_ids = (
        (later % grid_cols) * grid_rows + later // grid_cols
    ) * (2 * half_slots) + column_ids // devices
    later_ids = jnp.concatenate([later_ids, later_ids + half_slots])

    def panel_half(h):
        first = first_slot + h * half_slots
        rows = jnp.concatenate(
            [
                lax.dynamic_slice_in_dim(left_vecs, first, half_slots, 0),
                lax.dynamic_slice_in_dim(right_vecs, first, half_slots, 0),
            ],
            axis=0,
        )
        return gather_all(rows)

    def image_half(gathered, ids):
        raw = jnp.einsum("gfn,mn->gfm", matrices, gathered, preferred_element_type=jnp.float32)
        ordered = jnp.take(raw, ids, axis=2)
        feature_rows = ordered.shape[1]
        part = ordered.transpose(1, 0, 2).reshape(feature_rows, 4 * PANEL).astype(jnp.bfloat16)
        part = gather_prow(part)
        return lax.all_gather(part, "pcol", axis=0, tiled=True)

    slots = left_vecs.shape[0]
    height = PANEL // devices
    blocks = slots // (grid_rows * height)

    def slot_order(x):
        x = x.reshape(blocks, grid_rows, height, x.shape[1]).transpose(1, 0, 2, 3)
        return x.reshape(slots, x.shape[3])

    gathered_first = panel_half(0)
    gathered_second = panel_half(1)
    both_vecs = jnp.concatenate([left_vecs, right_vecs], axis=0)
    piece = image_half(gathered_first, pair_ids)
    panel_vecs = jnp.take(
        jnp.concatenate([gathered_first, gathered_second], axis=0),
        jnp.concatenate([pair_ids, pair_ids + gathered_first.shape[0]]),
        axis=0,
    )
    panel_prod = jnp.dot(panel_vecs, piece, preferred_element_type=jnp.float32)
    panel_top = combine(panel_prod[:PANEL], panel_prod[PANEL : 2 * PANEL])
    panel_bottom = combine(panel_prod[2 * PANEL : 3 * PANEL], panel_prod[3 * PANEL :])
    prod = jnp.dot(both_vecs, piece, preferred_element_type=jnp.float32)
    schur_first = slot_order(combine(prod[:slots], prod[slots:]))
    piece = image_half(gathered_second, later_ids)
    prod = jnp.dot(both_vecs, piece, preferred_element_type=jnp.float32)
    schur_second = slot_order(combine(prod[:slots], prod[slots:]))
    inverse = block_inverse_factor(panel_top)
    ahead = jnp.dot(
        panel_bottom,
        inverse.T,
        precision=lax.Precision.HIGH,
        preferred_element_type=jnp.float32,
    )
    place = jnp.arange(slots, dtype=jnp.int32)
    slot_of = (place % (blocks * height)) // height * (grid_rows * height) + (
        place // (blocks * height)
    ) * height + place % height
    schur_ids = slot_of * devices + residue
    full_t = lax.dot_general(
        inverse,
        schur_first,
        (((1,), (1,)), ((), ())),
        precision=lax.Precision.HIGH,
        preferred_element_type=jnp.float32,
    )
    full_t = jnp.where((schur_ids >= start)[None, :], full_t, jnp.float32(0.0))
    update_t = schur_second.T - jnp.dot(
        ahead, full_t, precision=lax.Precision.HIGH, preferred_element_type=jnp.float32
    )
    update_t = jnp.where((schur_ids >= start + PANEL)[None, :], update_t, jnp.float32(0.0))
    return relay_rows(full_t, update_t, owner_map, devices, grid_rows)


def solution(mesh):
    return jax.shard_map(
        body,
        mesh=mesh,
        in_specs=(
            P(("prow", "pcol"), None),
            P(("prow", "pcol"), None),
            P(("prow", "pcol"), None),
            P(("prow", "pcol"), None),
            P(),
            P(),
        ),
        out_specs=(P("pcol", "prow"), P("pcol", "prow")),
        check_vma=False,
    )
```
